768 devices in a mesh: slab: 48 (over x, z), tile: 16 (over y, core).
Axes of the slice: x: 4, y: 8, z: 12, core: 2. Of those that a mesh axis runs over, the one named last changes fastest.
Arguments:
- old_fine: float32 [49152, 5, 512], P(('slab', 'tile')), may hold values from -6 to 6
- coarse_fine: float32 [49152, 5, 64], P(('slab', 'tile')), may hold values from -6 to 6
- old_owner: int32 [48, 16, 64], P('slab', 'tile'), may hold values from 0 to 15, as said below
- new_refine: int32 [48, 16, 64], P('slab', 'tile'), may hold values from 0 to 1
- parent_map: int32 [48, 16, 64], P('slab', 'tile'), may hold values from 0 to 63
- courant: float32 [3, 5], replicated, may hold values from 0.05 to 0.3
Outputs:
- fine_next: float32 [5, 384, 512, 128], P(None, 'slab', 'tile')
The draws below stay inside these ranges and needn't reach their ends.
Inputs may be any that keep to these rules, and one draw needn't show every extreme that they name: `old_owner`: in each slab, old block k of tile t goes to tile (t + o_k) mod 16 with offsets o_k of the slab; every device sends exactly 4 blocks to each tile, and new slot k receives old slot k.
All inputs are finite; a program needn't handle non-finite values.
Results may differ from the reference program's by a relative error of at most 0.0003.
Values sent between devices are 32-bit elements; how exact they have to be, the bound alone decides.
No kernel may reach another device: no remote copies, remote signals or barrier semaphores. Data moves between devices by JAX's collectives and lax.ppermute only.
A program may use at most 64 MiB of HBM per device.

```python
import math
import jax
import jax.numpy as jnp
from jax import lax

F = 5
E = 8
BX = 16
BY = 4
K_DEV = 64
BLOCKS = 49152
N_SLAB = 48
N_TILE = 16


def draw_old_owner(key, part):
    per_peer = K_DEV // N_TILE
    keys = jax.random.split(key, N_SLAB)

    def one_slab(slab_key):
        first, second = jax.random.split(slab_key)
        order = jax.random.permutation(first, K_DEV)
        start = jax.random.randint(second, (), 0, N_TILE)
        return (order // per_peer + start) % N_TILE
    offsets = jax.vmap(one_slab)(keys)
    tiles = jnp.arange(N_TILE)[None, :, None]
    return ((tiles + offsets[:, None, :]) % N_TILE).astype(jnp.int32)


def draw_new_refine(key, part):
    first, second = jax.random.split(jax.random.fold_in(key, 7))
    limit = jax.random.randint(first, (N_SLAB, N_TILE, 1), 10, 70)
    rolls = jax.random.randint(second, (N_SLAB, N_TILE, K_DEV), 0, 100)
    return (rolls < limit).astype(jnp.int32)


def set_ends(values, stream_key, least, top_value):
    place = [jax.random.randint(jax.random.fold_in(stream_key, axis), (), 0, length) for axis, length in enumerate(values.shape)]
    widest = values.shape.index(max(values.shape))
    next_to = place[:widest] + [(place[widest] + 1) % values.shape[widest]] + place[widest + 1:]
    return values.at[tuple(place)].set(least).at[tuple(next_to)].set(top_value)


def block_scale(own_key, extent, cuts, low, high):
    loudness, own = 1.0, jax.random.fold_in(own_key, 6)
    for axis_at, blocks in cuts:
        heights = jnp.exp(jax.random.uniform(jax.random.fold_in(own, axis_at), (blocks,), jnp.float32, low / len(cuts), high / len(cuts)))
        loudness = loudness * jnp.repeat(heights, extent[axis_at] // blocks).reshape([-1 if axis == axis_at else 1 for axis in range(len(extent))])
    return loudness


def gaussian(key, extent, deviation, reach, pieces=(), kind=jnp.bfloat16):
    loudness = block_scale(key, extent, pieces, -0.22, 0.18) if pieces else 1.0
    values = jax.random.normal(key, extent, jnp.float32) * deviation * loudness
    return jnp.minimum(jnp.maximum(values, -reach), reach).astype(kind)


def setup_inputs(seed: int = 0) -> dict:
    arg_keys = jax.random.split(jax.random.key(seed), 7)
    old_fine = gaussian(arg_keys[0], (BLOCKS, F, E**3), 1.0, 6.0, ((0, 768),), jnp.float32)
    coarse_fine = gaussian(arg_keys[1], (BLOCKS, F, (E // 2)**3), 1.0, 6.0, ((0, 768),), jnp.float32)
    old_owner = draw_old_owner(jax.random.fold_in(arg_keys[6], 71), 0)
    new_refine = draw_new_refine(jax.random.fold_in(arg_keys[6], 71), 0)
    parent_map = set_ends(jax.random.randint(arg_keys[4], (N_SLAB, N_TILE, K_DEV), 0, K_DEV), jax.random.fold_in(arg_keys[4], 1), 0, K_DEV - 1).astype(jnp.int32)
    courant = jnp.clip(jnp.exp(jax.random.uniform(arg_keys[5], (3, F), jnp.float32, math.log(0.05), math.log(0.3))), 0.05, 0.3)
    return dict(old_fine=old_fine, coarse_fine=coarse_fine, old_owner=old_owner, new_refine=new_refine, parent_map=parent_map, courant=courant)


def minmod(left, right):
    return 0.5 * (jnp.sign(left) + jnp.sign(right)) * jnp.minimum(jnp.abs(left), jnp.abs(right))


def slopes(cells, axis):
    width = [(0, 0)] * cells.ndim
    width[axis] = (1, 1)
    padded = jnp.pad(cells, width, mode="edge")
    size = cells.shape[axis]
    below = lax.slice_in_dim(padded, 0, size, axis=axis)
    above = lax.slice_in_dim(padded, 2, size + 2, axis=axis)
    return minmod(cells - below, above - cells)


def refine_block(cells):
    nd = cells.ndim
    slope_z = slopes(cells, nd - 3)
    slope_y = slopes(cells, nd - 2)
    slope_x = slopes(cells, nd - 1)
    sigma = jnp.array([-0.25, 0.25], jnp.float32)
    def spread(v):
        return v[..., :, None, :, None, :, None]
    offset = (spread(slope_z) * sigma[:, None, None, None, None] + spread(slope_y) * sigma[:, None, None]) + spread(slope_x) * sigma
    fine = spread(cells) + offset
    half = cells.shape[-1]
    return fine.reshape(cells.shape[:-3] + (2 * half, 2 * half, 2 * half))


def advance(padded, courant):
    fields, zp, yp, xp = padded.shape
    zn, yn, xn = zp - 4, yp - 4, xp - 4
    def cut(dz, dy, dx):
        return padded[:, 2 + dz:2 + dz + zn, 2 + dy:2 + dy + yn, 2 + dx:2 + dx + xn]
    center = cut(0, 0, 0)
    total = jnp.zeros_like(center)
    for axis, unit in enumerate(((1, 0, 0), (0, 1, 0), (0, 0, 1))):
        lower1 = cut(-unit[0], -unit[1], -unit[2])
        lower2 = cut(-2 * unit[0], -2 * unit[1], -2 * unit[2])
        upper1 = cut(unit[0], unit[1], unit[2])
        face_hi = center + 0.5 * minmod(center - lower1, upper1 - center)
        face_lo = lower1 + 0.5 * minmod(lower1 - lower2, center - lower1)
        total = total + courant[axis][:, None, None, None] * (face_hi - face_lo)
    return center - total


def reference(old_fine, coarse_fine, old_owner, new_refine, parent_map, courant):
    slabs, tiles, blocks = old_owner.shape
    fields = old_fine.shape[1]
    half = E // 2
    old5 = old_fine.reshape(slabs, tiles, blocks, fields, E ** 3)
    offsets = old_owner[:, 0, :] % tiles
    source = (jnp.arange(tiles, dtype=jnp.int32)[None, :, None] - offsets[:, None, :]) % tiles
    slab_idx = jnp.arange(slabs, dtype=jnp.int32)[:, None, None]
    slot_idx = jnp.arange(blocks, dtype=jnp.int32)[None, None, :]
    moved = old5[slab_idx, source.astype(jnp.int32), slot_idx]
    coarse5 = coarse_fine.reshape(slabs, tiles, blocks, fields, half ** 3)
    rolled = jnp.roll(coarse5, 1, axis=0)
    parents = jnp.take_along_axis(rolled, parent_map.astype(jnp.int32)[:, :, :, None, None], axis=2)
    interp = refine_block(parents.reshape(slabs, tiles, blocks, fields, half, half, half)).reshape(slabs, tiles, blocks, fields, E ** 3)
    refilled = jnp.where((new_refine == 1)[:, :, :, None, None], interp, moved)
    region = refilled.reshape(slabs, tiles, BY, BX, fields, E, E, E)
    region = region.transpose(4, 0, 5, 1, 2, 6, 3, 7).reshape(fields, slabs * E, tiles * BY * E, BX * E)
    padded = jnp.pad(region, ((0, 0), (2, 2), (2, 2), (2, 2)))
    def one_slab(index):
        window = lax.dynamic_slice_in_dim(padded, (index * E).astype(jnp.int32), E + 4, axis=1)
        return advance(window, courant)
    stepped = lax.map(one_slab, jnp.arange(slabs, dtype=jnp.int32))
    return stepped.transpose(1, 0, 2, 3, 4).reshape(fields, slabs * E, tiles * BY * E, BX * E)
```

```python
import jax
import jax.numpy as jnp
from jax import lax
from jax.experimental import pallas as pl
from jax.experimental.pallas import tpu as pltpu
from jax.sharding import PartitionSpec as P

E = 8
BX = 16
BY = 4
INTERPRET = False


def minmod(left, right):
    return 0.5 * (jnp.sign(left) + jnp.sign(right)) * jnp.minimum(jnp.abs(left), jnp.abs(right))


def slopes(cells, axis):
    width = [(0, 0)] * cells.ndim
    width[axis] = (1, 1)
    padded = jnp.pad(cells, width, mode="edge")
    size = cells.shape[axis]
    below = lax.slice_in_dim(padded, 0, size, axis=axis)
    above = lax.slice_in_dim(padded, 2, size + 2, axis=axis)
    return minmod(cells - below, above - cells)


def refine_block(cells):
    nd = cells.ndim
    slope_z = slopes(cells, nd - 3)
    slope_y = slopes(cells, nd - 2)
    slope_x = slopes(cells, nd - 1)
    sigma = jnp.array([-0.25, 0.25], jnp.float32)

    def spread(value):
        return value[..., :, None, :, None, :, None]

    offset = (
        spread(slope_z) * sigma[:, None, None, None, None]
        + spread(slope_y) * sigma[:, None, None]
        + spread(slope_x) * sigma
    )
    fine = spread(cells) + offset
    half = cells.shape[-1]
    return fine.reshape(cells.shape[:-3] + (2 * half, 2 * half, 2 * half))


def assemble_kernel(arr_ref, int_ref, src_ref, o_ref, at_ref, p_ref):
    rows = at_ref.shape[1]
    lanes = src_ref.shape[1]

    @pl.when(pl.program_id(0) == 0)
    def _():
        row = lax.broadcasted_iota(jnp.int32, (rows, lanes), 0)
        lane = lax.broadcasted_iota(jnp.int32, (rows, lanes), 1)
        hit = row == src_ref[...]
        for x in range(E):
            sel = hit & (lane % E == x)
            p_ref[x * rows:(x + 1) * rows, :] = jnp.where(sel, 1.0, 0.0).astype(jnp.bfloat16)

    a = jnp.concatenate([arr_ref[0], int_ref[0]], axis=0)
    at_ref[...] = a.T
    zy = at_ref.shape[0] // E
    w = jnp.concatenate([at_ref[pl.ds(x, zy, stride=E), :] for x in range(E)], axis=1)
    hi = w.astype(jnp.bfloat16)
    rest = w - hi.astype(jnp.float32)
    mid = rest.astype(jnp.bfloat16)
    lo = (rest - mid.astype(jnp.float32)).astype(jnp.bfloat16)
    pm = p_ref[...]
    out = jnp.dot(hi, pm, preferred_element_type=jnp.float32)
    out = out + jnp.dot(mid, pm, preferred_element_type=jnp.float32)
    out = out + jnp.dot(lo, pm, preferred_element_type=jnp.float32)
    width = o_ref.shape[3]
    for by in range(o_ref.shape[2] // E):
        o_ref[0, :, by * E:(by + 1) * E, :] = out[:, by * width:(by + 1) * width].reshape(E, E, width)


def assemble(arrived, interp, srcrow):
    fields, blocks, cells = arrived.shape
    lanes = srcrow.shape[1]
    return pl.pallas_call(
        assemble_kernel,
        grid=(fields,),
        in_specs=[
            pl.BlockSpec((1, blocks, cells), lambda f: (f, 0, 0)),
            pl.BlockSpec((1, blocks, cells), lambda f: (f, 0, 0)),
            pl.BlockSpec((1, lanes), lambda f: (0, 0)),
        ],
        out_specs=pl.BlockSpec((1, E, BY * E, BX * E), lambda f: (f, 0, 0, 0)),
        out_shape=jax.ShapeDtypeStruct((fields, E, BY * E, BX * E), jnp.float32),
        scratch_shapes=[
            pltpu.VMEM((cells, 2 * blocks), jnp.float32),
            pltpu.VMEM((E * 2 * blocks, lanes), jnp.bfloat16),
        ],
        compiler_params=pltpu.CompilerParams(dimension_semantics=("arbitrary",)),
        interpret=INTERPRET,
    )(arrived, interp, srcrow)


def axis_terms(padded, axis, coef):
    size = padded.shape[axis] - 4

    def cut(d):
        return lax.slice_in_dim(padded, 2 + d, 2 + d + size, axis=axis)

    center = cut(0)
    lower1 = cut(-1)
    lower2 = cut(-2)
    upper1 = cut(1)
    face_hi = center + 0.5 * minmod(center - lower1, upper1 - center)
    face_lo = lower1 + 0.5 * minmod(lower1 - lower2, center - lower1)
    return coef[:, None, None, None] * (face_hi - face_lo)


def halo(block, axis, dim, width):
    count = lax.axis_size(axis)
    forward = [(i, i + 1) for i in range(count - 1)]
    backward = [(target, source) for source, target in forward]
    size = block.shape[dim]
    low = lax.ppermute(lax.slice_in_dim(block, size - width, size, axis=dim), axis, forward)
    high = lax.ppermute(lax.slice_in_dim(block, 0, width, axis=dim), axis, backward)
    return jnp.concatenate([low, block, high], axis=dim)


def local(old_fine, coarse_fine, old_owner, new_refine, parent_map, courant):
    slabs = lax.axis_size("slab")
    tiles = lax.axis_size("tile")
    myself = lax.axis_index("tile")
    blocks, fields, cells = old_fine.shape
    per_peer = blocks // tiles
    half = E // 2

    coarse_prev = lax.ppermute(coarse_fine, "slab", [(i, (i + 1) % slabs) for i in range(slabs)])

    owner = old_owner.reshape(-1)
    slot = jnp.arange(blocks, dtype=jnp.int32)
    same = owner[:, None] == owner[None, :]
    rank = jnp.sum((same & (slot[None, :] < slot[:, None])).astype(jnp.int32), axis=1)
    position = owner * per_peer + rank
    send_idx = jnp.sum(jnp.where(position[None, :] == slot[:, None], slot[None, :], 0), axis=1)
    outgoing = old_fine[send_idx]
    arrived = lax.all_to_all(outgoing, "tile", split_axis=0, concat_axis=0, tiled=True)
    source = (2 * myself - owner) % tiles
    inverse = source * per_peer + rank

    parents = coarse_prev[parent_map.reshape(-1)]
    interp = refine_block(parents.reshape(blocks, fields, half, half, half)).reshape(blocks, fields, cells)

    flags = new_refine.reshape(-1)
    src = jnp.where(flags == 1, blocks + slot, inverse)
    srcrow = jnp.repeat(src, E)[None, :]
    region = assemble(arrived.transpose(1, 0, 2), interp.transpose(1, 0, 2), srcrow)

    zpad = halo(region, "slab", 1, 2)
    ypad = halo(region, "tile", 2, 2)
    xpad = jnp.pad(region, ((0, 0), (0, 0), (0, 0), (2, 2)))
    total = axis_terms(zpad, 1, courant[0])
    total = total + axis_terms(ypad, 2, courant[1])
    total = total + axis_terms(xpad, 3, courant[2])
    return region - total


def solution(mesh):
    in_specs = (
        P(("slab", "tile"), None, None),
        P(("slab", "tile"), None, None),
        P("slab", "tile", None),
        P("slab", "tile", None),
        P("slab", "tile", None),
        P(),
    )
    out_specs = P(None, "slab", "tile", None)
    return jax.shard_map(local, mesh=mesh, in_specs=in_specs, out_specs=out_specs, check_vma=False)
```

```python
import jax
import jax.numpy as jnp
from jax import lax
from jax.experimental import pallas as pl
from jax.experimental.pallas import tpu as pltpu
from jax.sharding import PartitionSpec as P

E = 8
BX = 16
BY = 4
INTERPRET = False


def minmod(left, right):
    return 0.5 * (jnp.sign(left) + jnp.sign(right)) * jnp.minimum(jnp.abs(left), jnp.abs(right))


def slopes(cells, axis):
    width = [(0, 0)] * cells.ndim
    width[axis] = (1, 1)
    padded = jnp.pad(cells, width, mode="edge")
    size = cells.shape[axis]
    below = lax.slice_in_dim(padded, 0, size, axis=axis)
    above = lax.slice_in_dim(padded, 2, size + 2, axis=axis)
    return minmod(cells - below, above - cells)


def refine_block(cells):
    nd = cells.ndim
    slope_z = slopes(cells, nd - 3)
    slope_y = slopes(cells, nd - 2)
    slope_x = slopes(cells, nd - 1)
    sigma = jnp.array([-0.25, 0.25], jnp.float32)

    def spread(value):
        return value[..., :, None, :, None, :, None]

    offset = (
        spread(slope_z) * sigma[:, None, None, None, None]
        + spread(slope_y) * sigma[:, None, None]
        + spread(slope_x) * sigma
    )
    fine = spread(cells) + offset
    half = cells.shape[-1]
    return fine.reshape(cells.shape[:-3] + (2 * half, 2 * half, 2 * half))


def assemble_kernel(arr_ref, int_ref, src_ref, o_ref, at_ref, p_ref):
    rows = at_ref.shape[1]
    lanes = src_ref.shape[1]

    @pl.when(pl.program_id(0) == 0)
    def _():
        row = lax.broadcasted_iota(jnp.int32, (rows, lanes), 0)
        lane = lax.broadcasted_iota(jnp.int32, (rows, lanes), 1)
        hit = row == src_ref[...]
        for x in range(E):
            sel = hit & (lane % E == x)
            p_ref[x * rows:(x + 1) * rows, :] = jnp.where(sel, 1.0, 0.0).astype(jnp.bfloat16)

    a = jnp.concatenate([arr_ref[0], int_ref[0]], axis=0)
    at_ref[...] = a.T
    zy = at_ref.shape[0] // E
    w = jnp.concatenate([at_ref[pl.ds(x, zy, stride=E), :] for x in range(E)], axis=1)
    hi = w.astype(jnp.bfloat16)
    rest = w - hi.astype(jnp.float32)
    mid = rest.astype(jnp.bfloat16)
    lo = (rest - mid.astype(jnp.float32)).astype(jnp.bfloat16)
    pm = p_ref[...]
    out = jnp.dot(hi, pm, preferred_element_type=jnp.float32)
    out = out + jnp.dot(mid, pm, preferred_element_type=jnp.float32)
    out = out + jnp.dot(lo, pm, preferred_element_type=jnp.float32)
    width = o_ref.shape[3]
    for by in range(o_ref.shape[2] // E):
        o_ref[0, :, by * E:(by + 1) * E, :] = out[:, by * width:(by + 1) * width].reshape(E, E, width)


def assemble(arrived, interp, srcrow):
    fields, blocks, cells = arrived.shape
    lanes = srcrow.shape[1]
    return pl.pallas_call(
        assemble_kernel,
        grid=(fields,),
        in_specs=[
            pl.BlockSpec((1, blocks, cells), lambda f: (f, 0, 0)),
            pl.BlockSpec((1, blocks, cells), lambda f: (f, 0, 0)),
            pl.BlockSpec((1, lanes), lambda f: (0, 0)),
        ],
        out_specs=pl.BlockSpec((1, E, BY * E, BX * E), lambda f: (f, 0, 0, 0)),
        out_shape=jax.ShapeDtypeStruct((fields, E, BY * E, BX * E), jnp.float32),
        scratch_shapes=[
            pltpu.VMEM((cells, 2 * blocks), jnp.float32),
            pltpu.VMEM((E * 2 * blocks, lanes), jnp.bfloat16),
        ],
        compiler_params=pltpu.CompilerParams(dimension_semantics=("arbitrary",)),
        interpret=INTERPRET,
    )(arrived, interp, srcrow)


def axis_terms(padded, axis, coef):
    size = padded.shape[axis] - 4

    def cut(d):
        return lax.slice_in_dim(padded, 2 + d, 2 + d + size, axis=axis)

    center = cut(0)
    lower1 = cut(-1)
    lower2 = cut(-2)
    upper1 = cut(1)
    face_hi = center + 0.5 * minmod(center - lower1, upper1 - center)
    face_lo = lower1 + 0.5 * minmod(lower1 - lower2, center - lower1)
    return coef[:, None, None, None] * (face_hi - face_lo)


def halo(block, axis, dim, width):
    count = lax.axis_size(axis)
    forward = [(i, i + 1) for i in range(count - 1)]
    backward = [(target, source) for source, target in forward]
    size = block.shape[dim]
    low = lax.ppermute(lax.slice_in_dim(block, size - width, size, axis=dim), axis, forward)
    high = lax.ppermute(lax.slice_in_dim(block, 0, width, axis=dim), axis, backward)
    return jnp.concatenate([low, block, high], axis=dim)


def local(old_fine, coarse_fine, old_owner, new_refine, parent_map, courant):
    slabs = lax.axis_size("slab")
    tiles = lax.axis_size("tile")
    myself = lax.axis_index("tile")
    blocks, fields, cells = old_fine.shape
    per_peer = blocks // tiles
    half = E // 2

    coarse_prev = lax.ppermute(coarse_fine, "slab", [(i, (i + 1) % slabs) for i in range(slabs)])

    owner = old_owner.reshape(-1)
    slot = jnp.arange(blocks, dtype=jnp.int32)
    same = owner[:, None] == owner[None, :]
    rank = jnp.sum((same & (slot[None, :] < slot[:, None])).astype(jnp.int32), axis=1)
    position = owner * per_peer + rank
    send_idx = jnp.sum(jnp.where(position[None, :] == slot[:, None], slot[None, :], 0), axis=1)
    outgoing = old_fine[send_idx].reshape(tiles, per_peer * fields * cells // 128, 128)
    arrived = lax.all_to_all(outgoing, "tile", split_axis=0, concat_axis=0, tiled=True)
    arrived = arrived.reshape(blocks, fields, cells)
    source = (2 * myself - owner) % tiles
    inverse = source * per_peer + rank

    parents = coarse_prev[parent_map.reshape(-1)]
    interp = refine_block(parents.reshape(blocks, fields, half, half, half)).reshape(blocks, fields, cells)

    flags = new_refine.reshape(-1)
    src = jnp.where(flags == 1, blocks + slot, inverse)
    srcrow = jnp.repeat(src, E)[None, :]
    region = assemble(arrived.transpose(1, 0, 2), interp.transpose(1, 0, 2), srcrow)

    zpad = halo(region, "slab", 1, 2)
    ypad = halo(region, "tile", 2, 2)
    xpad = jnp.pad(region, ((0, 0), (0, 0), (0, 0), (2, 2)))
    total = axis_terms(zpad, 1, courant[0])
    total = total + axis_terms(ypad, 2, courant[1])
    total = total + axis_terms(xpad, 3, courant[2])
    return region - total


def solution(mesh):
    in_specs = (
        P(("slab", "tile"), None, None),
        P(("slab", "tile"), None, None),
        P("slab", "tile", None),
        P("slab", "tile", None),
        P("slab", "tile", None),
        P(),
    )
    out_specs = P(None, "slab", "tile", None)
    return jax.shard_map(local, mesh=mesh, in_specs=in_specs, out_specs=out_specs, check_vma=False)
```

```python
import jax
import jax.numpy as jnp
from jax import lax
from jax.experimental import pallas as pl
from jax.experimental.pallas import tpu as pltpu
from jax.sharding import PartitionSpec as P

E = 8
BX = 16
BY = 4
INTERPRET = False


def minmod(left, right):
    return 0.5 * (jnp.sign(left) + jnp.sign(right)) * jnp.minimum(jnp.abs(left), jnp.abs(right))


def slopes(cells, axis):
    width = [(0, 0)] * cells.ndim
    width[axis] = (1, 1)
    padded = jnp.pad(cells, width, mode="edge")
    size = cells.shape[axis]
    below = lax.slice_in_dim(padded, 0, size, axis=axis)
    above = lax.slice_in_dim(padded, 2, size + 2, axis=axis)
    return minmod(cells - below, above - cells)


def refine_block(cells):
    nd = cells.ndim
    slope_z = slopes(cells, nd - 3)
    slope_y = slopes(cells, nd - 2)
    slope_x = slopes(cells, nd - 1)
    sigma = jnp.array([-0.25, 0.25], jnp.float32)

    def spread(value):
        return value[..., :, None, :, None, :, None]

    offset = (
        spread(slope_z) * sigma[:, None, None, None, None]
        + spread(slope_y) * sigma[:, None, None]
        + spread(slope_x) * sigma
    )
    fine = spread(cells) + offset
    half = cells.shape[-1]
    return fine.reshape(cells.shape[:-3] + (2 * half, 2 * half, 2 * half))


def assemble_kernel(arr_ref, int_ref, src_ref, o_ref, zt_ref, zb_ref, yt_ref, yb_ref, at_ref, p_ref):
    rows = at_ref.shape[1]
    lanes = src_ref.shape[1]

    @pl.when(pl.program_id(0) == 0)
    def _():
        row = lax.broadcasted_iota(jnp.int32, (rows, lanes), 0)
        lane = lax.broadcasted_iota(jnp.int32, (rows, lanes), 1)
        hit = row == src_ref[...]
        for x in range(E):
            sel = hit & (lane % E == x)
            p_ref[x * rows:(x + 1) * rows, :] = jnp.where(sel, 1.0, 0.0).astype(jnp.bfloat16)

    a = jnp.concatenate([arr_ref[0], int_ref[0]], axis=0)
    at_ref[...] = a.T
    zy = at_ref.shape[0] // E
    w = jnp.concatenate([at_ref[pl.ds(x, zy, stride=E), :] for x in range(E)], axis=1)
    hi = w.astype(jnp.bfloat16)
    rest = w - hi.astype(jnp.float32)
    mid = rest.astype(jnp.bfloat16)
    lo = (rest - mid.astype(jnp.float32)).astype(jnp.bfloat16)
    pm = p_ref[...]
    out = jnp.dot(hi, pm, preferred_element_type=jnp.float32)
    out = out + jnp.dot(mid, pm, preferred_element_type=jnp.float32)
    out = out + jnp.dot(lo, pm, preferred_element_type=jnp.float32)
    width = o_ref.shape[3]
    count = o_ref.shape[2] // E
    for by in range(count):
        piece = out[:, by * width:(by + 1) * width].reshape(E, E, width)
        o_ref[0, :, by * E:(by + 1) * E, :] = piece
        zt_ref[0, :, by * E:(by + 1) * E, :] = piece[E - 2:]
        zb_ref[0, :, by * E:(by + 1) * E, :] = piece[:2]
        if by == 0:
            yb_ref[0] = piece[:, :2, :]
        if by == count - 1:
            yt_ref[0] = piece[:, E - 2:, :]


def assemble(arrived, interp, srcrow):
    fields, blocks, cells = arrived.shape
    lanes = srcrow.shape[1]
    return pl.pallas_call(
        assemble_kernel,
        grid=(fields,),
        in_specs=[
            pl.BlockSpec((1, blocks, cells), lambda f: (f, 0, 0)),
            pl.BlockSpec((1, blocks, cells), lambda f: (f, 0, 0)),
            pl.BlockSpec((1, lanes), lambda f: (0, 0)),
        ],
        out_specs=[
            pl.BlockSpec((1, E, BY * E, BX * E), lambda f: (f, 0, 0, 0)),
            pl.BlockSpec((1, 2, BY * E, BX * E), lambda f: (f, 0, 0, 0)),
            pl.BlockSpec((1, 2, BY * E, BX * E), lambda f: (f, 0, 0, 0)),
            pl.BlockSpec((1, E, 2, BX * E), lambda f: (f, 0, 0, 0)),
            pl.BlockSpec((1, E, 2, BX * E), lambda f: (f, 0, 0, 0)),
        ],
        out_shape=[
            jax.ShapeDtypeStruct((fields, E, BY * E, BX * E), jnp.float32),
            jax.ShapeDtypeStruct((fields, 2, BY * E, BX * E), jnp.float32),
            jax.ShapeDtypeStruct((fields, 2, BY * E, BX * E), jnp.float32),
            jax.ShapeDtypeStruct((fields, E, 2, BX * E), jnp.float32),
            jax.ShapeDtypeStruct((fields, E, 2, BX * E), jnp.float32),
        ],
        scratch_shapes=[
            pltpu.VMEM((cells, 2 * blocks), jnp.float32),
            pltpu.VMEM((E * 2 * blocks, lanes), jnp.bfloat16),
        ],
        compiler_params=pltpu.CompilerParams(dimension_semantics=("arbitrary",)),
        interpret=INTERPRET,
    )(arrived, interp, srcrow)


def kernel_minmod(left, right):
    def sgn(v):
        return jnp.where(v > 0, 1.0, 0.0) - jnp.where(v < 0, 1.0, 0.0)

    return 0.5 * (sgn(left) + sgn(right)) * jnp.minimum(jnp.abs(left), jnp.abs(right))


def kernel_term(center, lower1, lower2, upper1, coef):
    face_hi = center + 0.5 * kernel_minmod(center - lower1, upper1 - center)
    face_lo = lower1 + 0.5 * kernel_minmod(lower1 - lower2, center - lower1)
    return coef * (face_hi - face_lo)


def advance_kernel(c_ref, u_ref, zl_ref, zh_ref, yl_ref, yh_ref, o_ref, yp_ref):
    f = pl.program_id(0)
    u = u_ref[0]
    zn, yn, xn = u.shape
    zp = jnp.concatenate([zl_ref[0], u, zh_ref[0]], axis=0)
    tz = kernel_term(u, zp[1:zn + 1], zp[0:zn], zp[3:zn + 3], c_ref[0, f])
    yp_ref[:, E - 2:E, :] = yl_ref[0]
    yp_ref[:, E:E + yn, :] = u
    yp_ref[:, E + yn:E + yn + 2, :] = yh_ref[0]
    ty = kernel_term(u, yp_ref[:, E - 1:E - 1 + yn, :], yp_ref[:, E - 2:E - 2 + yn, :],
                     yp_ref[:, E + 1:E + 1 + yn, :], c_ref[1, f])
    lane = lax.broadcasted_iota(jnp.int32, u.shape, 2)
    lower1 = jnp.where(lane >= 1, pltpu.roll(u, 1, 2), 0.0)
    lower2 = jnp.where(lane >= 2, pltpu.roll(u, 2, 2), 0.0)
    upper1 = jnp.where(lane < xn - 1, pltpu.roll(u, xn - 1, 2), 0.0)
    tx = kernel_term(u, lower1, lower2, upper1, c_ref[2, f])
    o_ref[0] = u - ((tz + ty) + tx)


def advance(courant, region, zlo, zhi, ylo, yhi):
    fields, zn, yn, xn = region.shape
    return pl.pallas_call(
        advance_kernel,
        grid=(fields,),
        in_specs=[
            pl.BlockSpec(memory_space=pltpu.SMEM),
            pl.BlockSpec((1, zn, yn, xn), lambda f: (f, 0, 0, 0)),
            pl.BlockSpec((1, 2, yn, xn), lambda f: (f, 0, 0, 0)),
            pl.BlockSpec((1, 2, yn, xn), lambda f: (f, 0, 0, 0)),
            pl.BlockSpec((1, zn, 2, xn), lambda f: (f, 0, 0, 0)),
            pl.BlockSpec((1, zn, 2, xn), lambda f: (f, 0, 0, 0)),
        ],
        out_specs=pl.BlockSpec((1, zn, yn, xn), lambda f: (f, 0, 0, 0)),
        out_shape=jax.ShapeDtypeStruct(region.shape, jnp.float32),
        scratch_shapes=[pltpu.VMEM((zn, yn + 2 * E, xn), jnp.float32)],
        compiler_params=pltpu.CompilerParams(dimension_semantics=("arbitrary",)),
        interpret=INTERPRET,
    )(courant, region, zlo, zhi, ylo, yhi)


def axis_terms(padded, axis, coef):
    size = padded.shape[axis] - 4

    def cut(d):
        return lax.slice_in_dim(padded, 2 + d, 2 + d + size, axis=axis)

    center = cut(0)
    lower1 = cut(-1)
    lower2 = cut(-2)
    upper1 = cut(1)
    face_hi = center + 0.5 * minmod(center - lower1, upper1 - center)
    face_lo = lower1 + 0.5 * minmod(lower1 - lower2, center - lower1)
    return coef[:, None, None, None] * (face_hi - face_lo)


def halo(block, axis, dim, width):
    count = lax.axis_size(axis)
    forward = [(i, i + 1) for i in range(count - 1)]
    backward = [(target, source) for source, target in forward]
    size = block.shape[dim]
    low = lax.ppermute(lax.slice_in_dim(block, size - width, size, axis=dim), axis, forward)
    high = lax.ppermute(lax.slice_in_dim(block, 0, width, axis=dim), axis, backward)
    return jnp.concatenate([low, block, high], axis=dim)


def exchange(top, bottom, axis):
    count = lax.axis_size(axis)
    forward = [(i, i + 1) for i in range(count - 1)]
    backward = [(target, source) for source, target in forward]
    return lax.ppermute(top, axis, forward), lax.ppermute(bottom, axis, backward)


def local(old_fine, coarse_fine, old_owner, new_refine, parent_map, courant):
    slabs = lax.axis_size("slab")
    tiles = lax.axis_size("tile")
    myself = lax.axis_index("tile")
    blocks, fields, cells = old_fine.shape
    per_peer = blocks // tiles
    half = E // 2

    coarse_prev = lax.ppermute(coarse_fine, "slab", [(i, (i + 1) % slabs) for i in range(slabs)])

    owner = old_owner.reshape(-1)
    slot = jnp.arange(blocks, dtype=jnp.int32)
    same = owner[:, None] == owner[None, :]
    rank = jnp.sum((same & (slot[None, :] < slot[:, None])).astype(jnp.int32), axis=1)
    position = owner * per_peer + rank
    send_idx = jnp.sum(jnp.where(position[None, :] == slot[:, None], slot[None, :], 0), axis=1)
    outgoing = old_fine[send_idx].reshape(tiles, per_peer * fields * cells // 128, 128)
    arrived = lax.all_to_all(outgoing, "tile", split_axis=0, concat_axis=0, tiled=True)
    arrived = arrived.reshape(blocks, fields, cells)
    source = (2 * myself - owner) % tiles
    inverse = source * per_peer + rank

    parents = coarse_prev[parent_map.reshape(-1)]
    interp = refine_block(parents.reshape(blocks, fields, half, half, half)).reshape(blocks, fields, cells)

    flags = new_refine.reshape(-1)
    src = jnp.where(flags == 1, blocks + slot, inverse)
    srcrow = jnp.repeat(src, E)[None, :]
    region, ztop, zbot, ytop, ybot = assemble(arrived.transpose(1, 0, 2), interp.transpose(1, 0, 2), srcrow)

    zlo, zhi = exchange(ztop, zbot, "slab")
    ylo, yhi = exchange(ytop, ybot, "tile")
    return advance(courant, region, zlo, zhi, ylo, yhi)


def solution(mesh):
    in_specs = (
        P(("slab", "tile"), None, None),
        P(("slab", "tile"), None, None),
        P("slab", "tile", None),
        P("slab", "tile", None),
        P("slab", "tile", None),
        P(),
    )
    out_specs = P(None, "slab", "tile", None)
    return jax.shard_map(local, mesh=mesh, in_specs=in_specs, out_specs=out_specs, check_vma=False)
```

```python
import jax
import jax.numpy as jnp
from jax import lax
from jax.experimental import pallas as pl
from jax.experimental.pallas import tpu as pltpu
from jax.sharding import PartitionSpec as P

E = 8
BX = 16
BY = 4
INTERPRET = False


def minmod(left, right):
    return 0.5 * (jnp.sign(left) + jnp.sign(right)) * jnp.minimum(jnp.abs(left), jnp.abs(right))


def slopes(cells, axis):
    width = [(0, 0)] * cells.ndim
    width[axis] = (1, 1)
    padded = jnp.pad(cells, width, mode="edge")
    size = cells.shape[axis]
    below = lax.slice_in_dim(padded, 0, size, axis=axis)
    above = lax.slice_in_dim(padded, 2, size + 2, axis=axis)
    return minmod(cells - below, above - cells)


def refine_block(cells):
    nd = cells.ndim
    slope_z = slopes(cells, nd - 3)
    slope_y = slopes(cells, nd - 2)
    slope_x = slopes(cells, nd - 1)
    sigma = jnp.array([-0.25, 0.25], jnp.float32)

    def spread(value):
        return value[..., :, None, :, None, :, None]

    offset = (
        spread(slope_z) * sigma[:, None, None, None, None]
        + spread(slope_y) * sigma[:, None, None]
        + spread(slope_x) * sigma
    )
    fine = spread(cells) + offset
    half = cells.shape[-1]
    return fine.reshape(cells.shape[:-3] + (2 * half, 2 * half, 2 * half))


def assemble_kernel(arr_ref, int_ref, src_ref, o_ref, zt_ref, zb_ref, yt_ref, yb_ref, at_ref):
    fields, blocks, cells = arr_ref.shape
    rows = 2 * blocks
    lanes = src_ref.shape[1]
    zy = cells // E
    row = lax.broadcasted_iota(jnp.int32, (rows, lanes), 0)
    lane = lax.broadcasted_iota(jnp.int32, (rows, lanes), 1)
    hit = row == src_ref[...]
    pm = jnp.concatenate(
        [jnp.where(hit & (lane % E == x), 1.0, 0.0).astype(jnp.bfloat16) for x in range(E)], axis=0)
    parts = []
    for f in range(fields):
        a = jnp.concatenate([arr_ref[f], int_ref[f]], axis=0)
        at_ref[f * cells:(f + 1) * cells, :] = a.T
        parts.append(jnp.concatenate(
            [at_ref[pl.ds(f * cells + x, zy, stride=E), :] for x in range(E)], axis=1))
    w = jnp.concatenate(parts, axis=0)
    hi = w.astype(jnp.bfloat16)
    rest = w - hi.astype(jnp.float32)
    mid = rest.astype(jnp.bfloat16)
    lo = (rest - mid.astype(jnp.float32)).astype(jnp.bfloat16)
    res = jnp.dot(jnp.concatenate([hi, mid, lo], axis=0), pm, preferred_element_type=jnp.float32)
    n = fields * zy
    out = (res[:n] + res[n:2 * n]) + res[2 * n:]
    width = o_ref.shape[3]
    count = o_ref.shape[2] // E
    for f in range(fields):
        for by in range(count):
            piece = out[f * zy:(f + 1) * zy, by * width:(by + 1) * width].reshape(E, E, width)
            o_ref[f, :, by * E:(by + 1) * E, :] = piece
            zt_ref[f, :, by * E:(by + 1) * E, :] = piece[E - 2:]
            zb_ref[f, :, by * E:(by + 1) * E, :] = piece[:2]
            if by == 0:
                yb_ref[f] = piece[:, :2, :]
            if by == count - 1:
                yt_ref[f] = piece[:, E - 2:, :]


def assemble(arrived, interp, srcrow):
    fields, blocks, cells = arrived.shape
    return pl.pallas_call(
        assemble_kernel,
        out_shape=[
            jax.ShapeDtypeStruct((fields, E, BY * E, BX * E), jnp.float32),
            jax.ShapeDtypeStruct((fields, 2, BY * E, BX * E), jnp.float32),
            jax.ShapeDtypeStruct((fields, 2, BY * E, BX * E), jnp.float32),
            jax.ShapeDtypeStruct((fields, E, 2, BX * E), jnp.float32),
            jax.ShapeDtypeStruct((fields, E, 2, BX * E), jnp.float32),
        ],
        scratch_shapes=[pltpu.VMEM((fields * cells, 2 * blocks), jnp.float32)],
        interpret=INTERPRET,
    )(arrived, interp, srcrow)


def kernel_minmod(left, right):
    rising = (left > 0) & (right > 0)
    falling = (left < 0) & (right < 0)
    return jnp.where(rising, jnp.minimum(left, right), jnp.where(falling, jnp.maximum(left, right), 0.0))


def kernel_term(center, lower1, lower2, upper1, coef):
    face_hi = center + 0.5 * kernel_minmod(center - lower1, upper1 - center)
    face_lo = lower1 + 0.5 * kernel_minmod(lower1 - lower2, center - lower1)
    return coef * (face_hi - face_lo)


def advance_kernel(c_ref, u_ref, zl_ref, zh_ref, yl_ref, yh_ref, o_ref, yp_ref):
    f = pl.program_id(0)
    u = u_ref[0]
    zn, yn, xn = u.shape
    zp = jnp.concatenate([zl_ref[0], u, zh_ref[0]], axis=0)
    tz = kernel_term(u, zp[1:zn + 1], zp[0:zn], zp[3:zn + 3], c_ref[0, f])
    yp_ref[:, E - 2:E, :] = yl_ref[0]
    yp_ref[:, E:E + yn, :] = u
    yp_ref[:, E + yn:E + yn + 2, :] = yh_ref[0]
    ty = kernel_term(u, yp_ref[:, E - 1:E - 1 + yn, :], yp_ref[:, E - 2:E - 2 + yn, :],
                     yp_ref[:, E + 1:E + 1 + yn, :], c_ref[1, f])
    lane = lax.broadcasted_iota(jnp.int32, u.shape, 2)
    lower1 = jnp.where(lane >= 1, pltpu.roll(u, 1, 2), 0.0)
    lower2 = jnp.where(lane >= 2, pltpu.roll(u, 2, 2), 0.0)
    upper1 = jnp.where(lane < xn - 1, pltpu.roll(u, xn - 1, 2), 0.0)
    tx = kernel_term(u, lower1, lower2, upper1, c_ref[2, f])
    o_ref[0] = u - ((tz + ty) + tx)


def advance(courant, region, zlo, zhi, ylo, yhi):
    fields, zn, yn, xn = region.shape
    return pl.pallas_call(
        advance_kernel,
        grid=(fields,),
        in_specs=[
            pl.BlockSpec(memory_space=pltpu.SMEM),
            pl.BlockSpec((1, zn, yn, xn), lambda f: (f, 0, 0, 0)),
            pl.BlockSpec((1, 2, yn, xn), lambda f: (f, 0, 0, 0)),
            pl.BlockSpec((1, 2, yn, xn), lambda f: (f, 0, 0, 0)),
            pl.BlockSpec((1, zn, 2, xn), lambda f: (f, 0, 0, 0)),
            pl.BlockSpec((1, zn, 2, xn), lambda f: (f, 0, 0, 0)),
        ],
        out_specs=pl.BlockSpec((1, zn, yn, xn), lambda f: (f, 0, 0, 0)),
        out_shape=jax.ShapeDtypeStruct(region.shape, jnp.float32),
        scratch_shapes=[pltpu.VMEM((zn, yn + 2 * E, xn), jnp.float32)],
        compiler_params=pltpu.CompilerParams(dimension_semantics=("arbitrary",)),
        interpret=INTERPRET,
    )(courant, region, zlo, zhi, ylo, yhi)


def exchange(top, bottom, axis):
    count = lax.axis_size(axis)
    forward = [(i, i + 1) for i in range(count - 1)]
    backward = [(target, source) for source, target in forward]
    return lax.ppermute(top, axis, forward), lax.ppermute(bottom, axis, backward)


def local(old_fine, coarse_fine, old_owner, new_refine, parent_map, courant):
    slabs = lax.axis_size("slab")
    tiles = lax.axis_size("tile")
    myself = lax.axis_index("tile")
    blocks, fields, cells = old_fine.shape
    per_peer = blocks // tiles
    half = E // 2

    coarse_prev = lax.ppermute(coarse_fine, "slab", [(i, (i + 1) % slabs) for i in range(slabs)])

    owner = old_owner.reshape(-1)
    slot = jnp.arange(blocks, dtype=jnp.int32)
    same = owner[:, None] == owner[None, :]
    rank = jnp.sum((same & (slot[None, :] < slot[:, None])).astype(jnp.int32), axis=1)
    position = owner * per_peer + rank
    send_idx = jnp.sum(jnp.where(position[None, :] == slot[:, None], slot[None, :], 0), axis=1)
    outgoing = old_fine[send_idx].reshape(tiles, per_peer * fields * cells // 128, 128)
    arrived = lax.all_to_all(outgoing, "tile", split_axis=0, concat_axis=0, tiled=True)
    arrived = arrived.reshape(blocks, fields, cells)
    source = (2 * myself - owner) % tiles
    inverse = source * per_peer + rank

    parents = coarse_prev[parent_map.reshape(-1)]
    interp = refine_block(parents.reshape(blocks, fields, half, half, half)).reshape(blocks, fields, cells)

    flags = new_refine.reshape(-1)
    src = jnp.where(flags == 1, blocks + slot, inverse)
    srcrow = jnp.repeat(src, E)[None, :]
    region, ztop, zbot, ytop, ybot = assemble(arrived.transpose(1, 0, 2), interp.transpose(1, 0, 2), srcrow)

    zlo, zhi = exchange(ztop, zbot, "slab")
    ylo, yhi = exchange(ytop, ybot, "tile")
    return advance(courant, region, zlo, zhi, ylo, yhi)


def solution(mesh):
    in_specs = (
        P(("slab", "tile"), None, None),
        P(("slab", "tile"), None, None),
        P("slab", "tile", None),
        P("slab", "tile", None),
        P("slab", "tile", None),
        P(),
    )
    out_specs = P(None, "slab", "tile", None)
    return jax.shard_map(local, mesh=mesh, in_specs=in_specs, out_specs=out_specs, check_vma=False)
```

```python
import jax
import jax.numpy as jnp
from jax import lax
from jax.experimental import pallas as pl
from jax.experimental.pallas import tpu as pltpu
from jax.sharding import PartitionSpec as P

E = 8
BX = 16
BY = 4
INTERPRET = False


def minmod(left, right):
    return 0.5 * (jnp.sign(left) + jnp.sign(right)) * jnp.minimum(jnp.abs(left), jnp.abs(right))


def slopes(cells, axis):
    width = [(0, 0)] * cells.ndim
    width[axis] = (1, 1)
    padded = jnp.pad(cells, width, mode="edge")
    size = cells.shape[axis]
    below = lax.slice_in_dim(padded, 0, size, axis=axis)
    above = lax.slice_in_dim(padded, 2, size + 2, axis=axis)
    return minmod(cells - below, above - cells)


def refine_block(cells):
    nd = cells.ndim
    slope_z = slopes(cells, nd - 3)
    slope_y = slopes(cells, nd - 2)
    slope_x = slopes(cells, nd - 1)
    sigma = jnp.array([-0.25, 0.25], jnp.float32)

    def spread(value):
        return value[..., :, None, :, None, :, None]

    offset = (
        spread(slope_z) * sigma[:, None, None, None, None]
        + spread(slope_y) * sigma[:, None, None]
        + spread(slope_x) * sigma
    )
    fine = spread(cells) + offset
    half = cells.shape[-1]
    return fine.reshape(cells.shape[:-3] + (2 * half, 2 * half, 2 * half))


def assemble_kernel(arr_ref, int_ref, p_ref, o_ref, zt_ref, zb_ref, yt_ref, yb_ref, at_ref):
    fields, blocks, cells = int_ref.shape
    stride = arr_ref.shape[0] // blocks
    quarters = cells // arr_ref.shape[1]
    zy = cells // E
    parts = []
    for f in range(fields):
        moved = jnp.concatenate(
            [arr_ref[pl.ds(f * quarters + q, blocks, stride=stride), :] for q in range(quarters)], axis=1)
        a = jnp.concatenate([moved, int_ref[f]], axis=0)
        at_ref[f * cells:(f + 1) * cells, :] = a.T
        parts.append(jnp.concatenate(
            [at_ref[pl.ds(f * cells + x, zy, stride=E), :] for x in range(E)], axis=1))
    w = jnp.concatenate(parts, axis=0)
    hi = w.astype(jnp.bfloat16)
    rest = w - hi.astype(jnp.float32)
    mid = rest.astype(jnp.bfloat16)
    lo = (rest - mid.astype(jnp.float32)).astype(jnp.bfloat16)
    res = jnp.dot(jnp.concatenate([hi, mid, lo], axis=0), p_ref[...], preferred_element_type=jnp.float32)
    n = fields * zy
    out = (res[:n] + res[n:2 * n]) + res[2 * n:]
    width = o_ref.shape[3]
    count = o_ref.shape[2] // E
    for f in range(fields):
        for by in range(count):
            piece = out[f * zy:(f + 1) * zy, by * width:(by + 1) * width].reshape(E, E, width)
            o_ref[f, :, by * E:(by + 1) * E, :] = piece
            zt_ref[f, :, by * E:(by + 1) * E, :] = piece[E - 2:]
            zb_ref[f, :, by * E:(by + 1) * E, :] = piece[:2]
            if by == 0:
                yb_ref[f] = piece[:, :2, :]
            if by == count - 1:
                yt_ref[f] = piece[:, E - 2:, :]


def assemble(arrived, interp, onehot):
    fields, blocks, cells = interp.shape
    return pl.pallas_call(
        assemble_kernel,
        out_shape=[
            jax.ShapeDtypeStruct((fields, E, BY * E, BX * E), jnp.float32),
            jax.ShapeDtypeStruct((fields, 2, BY * E, BX * E), jnp.float32),
            jax.ShapeDtypeStruct((fields, 2, BY * E, BX * E), jnp.float32),
            jax.ShapeDtypeStruct((fields, E, 2, BX * E), jnp.float32),
            jax.ShapeDtypeStruct((fields, E, 2, BX * E), jnp.float32),
        ],
        scratch_shapes=[pltpu.VMEM((fields * cells, 2 * blocks), jnp.float32)],
        interpret=INTERPRET,
    )(arrived, interp, onehot)


def kernel_minmod(left, right):
    rising = (left > 0) & (right > 0)
    falling = (left < 0) & (right < 0)
    return jnp.where(rising, jnp.minimum(left, right), jnp.where(falling, jnp.maximum(left, right), 0.0))


def face(below, cell, above):
    return cell + 0.5 * kernel_minmod(cell - below, above - cell)


def advance_kernel(c_ref, u_ref, zl_ref, zh_ref, yl_ref, yh_ref, o_ref, yp_ref, g_ref):
    f = pl.program_id(0)
    u = u_ref[0]
    zn, yn, xn = u.shape
    zp = jnp.concatenate([zl_ref[0], u, zh_ref[0]], axis=0)
    gz = face(zp[0:zn + 1], zp[1:zn + 2], zp[2:zn + 3])
    tz = c_ref[0, f] * (gz[1:] - gz[:-1])
    yp_ref[:, E - 2:E, :] = yl_ref[0]
    yp_ref[:, E:E + yn, :] = u
    yp_ref[:, E + yn:E + yn + 2, :] = yh_ref[0]
    span = g_ref.shape[1]
    g_ref[...] = face(yp_ref[:, E - 2:E - 2 + span, :], yp_ref[:, E - 1:E - 1 + span, :],
                      yp_ref[:, E:E + span, :])
    ty = c_ref[1, f] * (g_ref[:, 1:yn + 1, :] - g_ref[:, 0:yn, :])
    lane = lax.broadcasted_iota(jnp.int32, u.shape, 2)
    lower1 = jnp.where(lane >= 1, pltpu.roll(u, 1, 2), 0.0)
    upper1 = jnp.where(lane < xn - 1, pltpu.roll(u, xn - 1, 2), 0.0)
    gx = face(lower1, u, upper1)
    gx_lo = jnp.where(lane >= 1, pltpu.roll(gx, 1, 2), 0.0)
    tx = c_ref[2, f] * (gx - gx_lo)
    o_ref[0] = u - ((tz + ty) + tx)


def advance(courant, region, zlo, zhi, ylo, yhi):
    fields, zn, yn, xn = region.shape
    return pl.pallas_call(
        advance_kernel,
        grid=(fields,),
        in_specs=[
            pl.BlockSpec(memory_space=pltpu.SMEM),
            pl.BlockSpec((1, zn, yn, xn), lambda f: (f, 0, 0, 0)),
            pl.BlockSpec((1, 2, yn, xn), lambda f: (f, 0, 0, 0)),
            pl.BlockSpec((1, 2, yn, xn), lambda f: (f, 0, 0, 0)),
            pl.BlockSpec((1, zn, 2, xn), lambda f: (f, 0, 0, 0)),
            pl.BlockSpec((1, zn, 2, xn), lambda f: (f, 0, 0, 0)),
        ],
        out_specs=pl.BlockSpec((1, zn, yn, xn), lambda f: (f, 0, 0, 0)),
        out_shape=jax.ShapeDtypeStruct(region.shape, jnp.float32),
        scratch_shapes=[
            pltpu.VMEM((zn, yn + 2 * E, xn), jnp.float32),
            pltpu.VMEM((zn, yn + E, xn), jnp.float32),
        ],
        compiler_params=pltpu.CompilerParams(dimension_semantics=("arbitrary",)),
        interpret=INTERPRET,
    )(courant, region, zlo, zhi, ylo, yhi)


def exchange(top, bottom, axis):
    count = lax.axis_size(axis)
    forward = [(i, i + 1) for i in range(count - 1)]
    backward = [(target, source) for source, target in forward]
    return lax.ppermute(top, axis, forward), lax.ppermute(bottom, axis, backward)


def local(old_fine, coarse_fine, old_owner, new_refine, parent_map, courant):
    slabs = lax.axis_size("slab")
    tiles = lax.axis_size("tile")
    myself = lax.axis_index("tile")
    blocks, fields, cells = old_fine.shape
    per_peer = blocks // tiles
    half = E // 2

    coarse_prev = lax.ppermute(coarse_fine, "slab", [(i, (i + 1) % slabs) for i in range(slabs)])

    owner = old_owner.reshape(-1)
    slot = jnp.arange(blocks, dtype=jnp.int32)
    same = owner[:, None] == owner[None, :]
    rank = jnp.sum((same & (slot[None, :] < slot[:, None])).astype(jnp.int32), axis=1)
    position = owner * per_peer + rank
    send_idx = jnp.sum(jnp.where(position[None, :] == slot[:, None], slot[None, :], 0), axis=1)
    outgoing = old_fine[send_idx].reshape(tiles, per_peer * fields * cells // 128, 128)
    arrived = lax.all_to_all(outgoing, "tile", split_axis=0, concat_axis=0, tiled=True)
    arrived = arrived.reshape(-1, 128)
    source = (2 * myself - owner) % tiles
    inverse = source * per_peer + rank

    parents = coarse_prev[parent_map.reshape(-1)]
    interp = refine_block(parents.reshape(blocks, fields, half, half, half)).reshape(blocks, fields, cells)

    flags = new_refine.reshape(-1)
    src = jnp.where(flags == 1, blocks + slot, inverse)
    lane = jnp.arange(blocks * E, dtype=jnp.int32)
    row = jnp.arange(2 * blocks, dtype=jnp.int32)
    hit = (row[None, :, None] == src[lane // E][None, None, :]) & (
        lane[None, None, :] % E == jnp.arange(E, dtype=jnp.int32)[:, None, None])
    onehot = hit.astype(jnp.bfloat16).reshape(E * 2 * blocks, blocks * E)
    region, ztop, zbot, ytop, ybot = assemble(arrived, interp.transpose(1, 0, 2), onehot)

    zlo, zhi = exchange(ztop, zbot, "slab")
    ylo, yhi = exchange(ytop, ybot, "tile")
    return advance(courant, region, zlo, zhi, ylo, yhi)


def solution(mesh):
    in_specs = (
        P(("slab", "tile"), None, None),
        P(("slab", "tile"), None, None),
        P("slab", "tile", None),
        P("slab", "tile", None),
        P("slab", "tile", None),
        P(),
    )
    out_specs = P(None, "slab", "tile", None)
    return jax.shard_map(local, mesh=mesh, in_specs=in_specs, out_specs=out_specs, check_vma=False)
```

```python
import jax
import jax.numpy as jnp
from jax import lax
from jax.experimental import pallas as pl
from jax.experimental.pallas import tpu as pltpu
from jax.sharding import PartitionSpec as P

E = 8
BX = 16
BY = 4
INTERPRET = False


def minmod(left, right):
    return 0.5 * (jnp.sign(left) + jnp.sign(right)) * jnp.minimum(jnp.abs(left), jnp.abs(right))


def slopes(cells, axis):
    width = [(0, 0)] * cells.ndim
    width[axis] = (1, 1)
    padded = jnp.pad(cells, width, mode="edge")
    size = cells.shape[axis]
    below = lax.slice_in_dim(padded, 0, size, axis=axis)
    above = lax.slice_in_dim(padded, 2, size + 2, axis=axis)
    return minmod(cells - below, above - cells)


def refine_block(cells):
    nd = cells.ndim
    slope_z = slopes(cells, nd - 3)
    slope_y = slopes(cells, nd - 2)
    slope_x = slopes(cells, nd - 1)
    sigma = jnp.array([-0.25, 0.25], jnp.float32)

    def spread(value):
        return value[..., :, None, :, None, :, None]

    offset = (
        spread(slope_z) * sigma[:, None, None, None, None]
        + spread(slope_y) * sigma[:, None, None]
        + spread(slope_x) * sigma
    )
    fine = spread(cells) + offset
    half = cells.shape[-1]
    return fine.reshape(cells.shape[:-3] + (2 * half, 2 * half, 2 * half))


def assemble_kernel(arr_ref, int_ref, p_ref, o_ref, zt_ref, zb_ref, yt_ref, yb_ref, at_ref):
    fields, blocks, cells = int_ref.shape
    stride = arr_ref.shape[0] // blocks
    quarters = cells // arr_ref.shape[1]
    zy = cells // E
    parts = []
    for f in range(fields):
        moved = jnp.concatenate(
            [arr_ref[pl.ds(f * quarters + q, blocks, stride=stride), :] for q in range(quarters)], axis=1)
        a = jnp.concatenate([moved, int_ref[f]], axis=0)
        at_ref[f * cells:(f + 1) * cells, :] = a.T
        parts.append(jnp.concatenate(
            [at_ref[pl.ds(f * cells + x, zy, stride=E), :] for x in range(E)], axis=1))
    w = jnp.concatenate(parts, axis=0)
    hi = w.astype(jnp.bfloat16)
    rest = w - hi.astype(jnp.float32)
    mid = rest.astype(jnp.bfloat16)
    lo = (rest - mid.astype(jnp.float32)).astype(jnp.bfloat16)
    res = jnp.dot(jnp.concatenate([hi, mid, lo], axis=0), p_ref[...], preferred_element_type=jnp.float32)
    n = fields * zy
    out = (res[:n] + res[n:2 * n]) + res[2 * n:]
    width = o_ref.shape[3]
    count = o_ref.shape[2] // E
    for f in range(fields):
        for by in range(count):
            piece = out[f * zy:(f + 1) * zy, by * width:(by + 1) * width].reshape(E, E, width)
            o_ref[f, :, by * E:(by + 1) * E, :] = piece
            zt_ref[f, :, by * E:(by + 1) * E, :] = piece[E - 2:]
            zb_ref[f, :, by * E:(by + 1) * E, :] = piece[:2]
            if by == 0:
                yb_ref[f] = piece[:, :2, :]
            if by == count - 1:
                yt_ref[f] = piece[:, E - 2:, :]


def onehot_kernel(src_ref, p_ref):
    rows = p_ref.shape[0] // E
    lanes = src_ref.shape[1]
    row = lax.broadcasted_iota(jnp.int32, (rows, lanes), 0)
    lane = lax.broadcasted_iota(jnp.int32, (rows, lanes), 1)
    hit = row == src_ref[...]
    for x in range(E):
        sel = hit & (lane % E == x)
        p_ref[x * rows:(x + 1) * rows, :] = jnp.where(sel, 1.0, 0.0).astype(jnp.bfloat16)


def build_onehot(srcrow, rows):
    lanes = srcrow.shape[1]
    return pl.pallas_call(
        onehot_kernel,
        out_shape=jax.ShapeDtypeStruct((E * rows, lanes), jnp.bfloat16),
        interpret=INTERPRET,
    )(srcrow)


def assemble(arrived, interp, onehot):
    fields, blocks, cells = interp.shape
    return pl.pallas_call(
        assemble_kernel,
        out_shape=[
            jax.ShapeDtypeStruct((fields, E, BY * E, BX * E), jnp.float32),
            jax.ShapeDtypeStruct((fields, 2, BY * E, BX * E), jnp.float32),
            jax.ShapeDtypeStruct((fields, 2, BY * E, BX * E), jnp.float32),
            jax.ShapeDtypeStruct((fields, E, 2, BX * E), jnp.float32),
            jax.ShapeDtypeStruct((fields, E, 2, BX * E), jnp.float32),
        ],
        scratch_shapes=[pltpu.VMEM((fields * cells, 2 * blocks), jnp.float32)],
        interpret=INTERPRET,
    )(arrived, interp, onehot)


def kernel_minmod(left, right):
    rising = (left > 0) & (right > 0)
    falling = (left < 0) & (right < 0)
    return jnp.where(rising, jnp.minimum(left, right), jnp.where(falling, jnp.maximum(left, right), 0.0))


def face(below, cell, above):
    return cell + 0.5 * kernel_minmod(cell - below, above - cell)


def advance_kernel(c_ref, u_ref, zl_ref, zh_ref, yl_ref, yh_ref, o_ref, yp_ref, g_ref):
    f = pl.program_id(0)
    zn, yn, xn = u_ref.shape[1:]
    cz = c_ref[0, f]
    cy = c_ref[1, f]
    cx = c_ref[2, f]
    yp_ref[:, E - 2:E, :] = yl_ref[0]
    yp_ref[:, E:E + yn, :] = u_ref[0]
    yp_ref[:, E + yn:E + yn + 2, :] = yh_ref[0]
    span = g_ref.shape[0]
    lane = lax.broadcasted_iota(jnp.int32, (yn, xn), 1)

    def plane(j):
        if j < 2:
            return zl_ref[0, j]
        if j < zn + 2:
            return u_ref[0, j - 2]
        return zh_ref[0, j - zn - 2]

    g_prev = face(plane(0), plane(1), plane(2))
    for z in range(zn):
        u = plane(z + 2)
        g_next = face(plane(z + 1), u, plane(z + 3))
        tz = cz * (g_next - g_prev)
        g_prev = g_next
        g_ref[...] = face(yp_ref[z, E - 2:E - 2 + span, :], yp_ref[z, E - 1:E - 1 + span, :],
                          yp_ref[z, E:E + span, :])
        ty = cy * (g_ref[1:yn + 1, :] - g_ref[0:yn, :])
        lower1 = jnp.where(lane >= 1, pltpu.roll(u, 1, 1), 0.0)
        upper1 = jnp.where(lane < xn - 1, pltpu.roll(u, xn - 1, 1), 0.0)
        gx = face(lower1, u, upper1)
        gx_lo = jnp.where(lane >= 1, pltpu.roll(gx, 1, 1), 0.0)
        tx = cx * (gx - gx_lo)
        o_ref[0, z] = u - ((tz + ty) + tx)


def advance(courant, region, zlo, zhi, ylo, yhi):
    fields, zn, yn, xn = region.shape
    return pl.pallas_call(
        advance_kernel,
        grid=(fields,),
        in_specs=[
            pl.BlockSpec(memory_space=pltpu.SMEM),
            pl.BlockSpec((1, zn, yn, xn), lambda f: (f, 0, 0, 0)),
            pl.BlockSpec((1, 2, yn, xn), lambda f: (f, 0, 0, 0)),
            pl.BlockSpec((1, 2, yn, xn), lambda f: (f, 0, 0, 0)),
            pl.BlockSpec((1, zn, 2, xn), lambda f: (f, 0, 0, 0)),
            pl.BlockSpec((1, zn, 2, xn), lambda f: (f, 0, 0, 0)),
        ],
        out_specs=pl.BlockSpec((1, zn, yn, xn), lambda f: (f, 0, 0, 0)),
        out_shape=jax.ShapeDtypeStruct(region.shape, jnp.float32),
        scratch_shapes=[
            pltpu.VMEM((zn, yn + 2 * E, xn), jnp.float32),
            pltpu.VMEM((yn + E, xn), jnp.float32),
        ],
        compiler_params=pltpu.CompilerParams(dimension_semantics=("arbitrary",)),
        interpret=INTERPRET,
    )(courant, region, zlo, zhi, ylo, yhi)


def exchange(top, bottom, axis):
    count = lax.axis_size(axis)
    forward = [(i, i + 1) for i in range(count - 1)]
    backward = [(target, source) for source, target in forward]
    return lax.ppermute(top, axis, forward), lax.ppermute(bottom, axis, backward)


def local(old_fine, coarse_fine, old_owner, new_refine, parent_map, courant):
    slabs = lax.axis_size("slab")
    tiles = lax.axis_size("tile")
    myself = lax.axis_index("tile")
    blocks, fields, cells = old_fine.shape
    per_peer = blocks // tiles
    half = E // 2

    coarse_prev = lax.ppermute(coarse_fine, "slab", [(i, (i + 1) % slabs) for i in range(slabs)])

    owner = old_owner.reshape(-1)
    slot = jnp.arange(blocks, dtype=jnp.int32)
    same = owner[:, None] == owner[None, :]
    rank = jnp.sum((same & (slot[None, :] < slot[:, None])).astype(jnp.int32), axis=1)
    position = owner * per_peer + rank
    send_idx = jnp.sum(jnp.where(position[None, :] == slot[:, None], slot[None, :], 0), axis=1)
    outgoing = old_fine[send_idx].reshape(tiles, per_peer * fields * cells // 128, 128)
    arrived = lax.all_to_all(outgoing, "tile", split_axis=0, concat_axis=0, tiled=True)
    arrived = arrived.reshape(-1, 128)
    source = (2 * myself - owner) % tiles
    inverse = source * per_peer + rank

    parents = coarse_prev[parent_map.reshape(-1)]
    interp = refine_block(parents.reshape(blocks, fields, half, half, half)).reshape(blocks, fields, cells)

    flags = new_refine.reshape(-1)
    src = jnp.where(flags == 1, blocks + slot, inverse)
    onehot = build_onehot(jnp.repeat(src, E)[None, :], 2 * blocks)
    region, ztop, zbot, ytop, ybot = assemble(arrived, interp.transpose(1, 0, 2), onehot)

    zlo, zhi = exchange(ztop, zbot, "slab")
    ylo, yhi = exchange(ytop, ybot, "tile")
    return advance(courant, region, zlo, zhi, ylo, yhi)


def solution(mesh):
    in_specs = (
        P(("slab", "tile"), None, None),
        P(("slab", "tile"), None, None),
        P("slab", "tile", None),
        P("slab", "tile", None),
        P("slab", "tile", None),
        P(),
    )
    out_specs = P(None, "slab", "tile", None)
    return jax.shard_map(local, mesh=mesh, in_specs=in_specs, out_specs=out_specs, check_vma=False)
```

```python
import jax
import jax.numpy as jnp
from jax import lax
from jax.experimental import pallas as pl
from jax.experimental.pallas import tpu as pltpu
from jax.sharding import PartitionSpec as P

E = 8
BX = 16
BY = 4
INTERPRET = False


def minmod(left, right):
    return 0.5 * (jnp.sign(left) + jnp.sign(right)) * jnp.minimum(jnp.abs(left), jnp.abs(right))


def slopes_kt(cells, axis):
    width = [(0, 0)] * cells.ndim
    width[axis] = (1, 1)
    padded = jnp.pad(cells, width, mode="edge")
    size = cells.shape[axis]
    below = lax.slice_in_dim(padded, 0, size, axis=axis)
    above = lax.slice_in_dim(padded, 2, size + 2, axis=axis)
    return minmod(cells - below, above - cells)


def refine_block_kt(cells):
    nd = cells.ndim
    slope_z = slopes_kt(cells, nd - 4)
    slope_y = slopes_kt(cells, nd - 3)
    slope_x = slopes_kt(cells, nd - 2)
    sigma = jnp.array([-0.25, 0.25], jnp.float32)

    def spread(value):
        return value[..., :, None, :, None, :, None, :]

    offset = (
        spread(slope_z) * sigma[:, None, None, None, None, None]
        + spread(slope_y) * sigma[:, None, None, None]
        + spread(slope_x) * sigma[:, None]
    )
    fine = spread(cells) + offset
    half = cells.shape[-2]
    return fine.reshape(cells.shape[:-4] + ((2 * half) ** 3, cells.shape[-1]))


def assemble_kernel(arr_ref, int_ref, p_ref, o_ref, zt_ref, zb_ref, yt_ref, yb_ref, at_ref):
    fields, cells, blocks = int_ref.shape
    stride = arr_ref.shape[0] // blocks
    quarters = cells // arr_ref.shape[1]
    zy = cells // E
    parts = []
    for f in range(fields):
        moved = jnp.concatenate(
            [arr_ref[pl.ds(f * quarters + q, blocks, stride=stride), :] for q in range(quarters)], axis=1)
        a = jnp.concatenate([moved, jnp.zeros_like(moved)], axis=0)
        at_ref[f * cells:(f + 1) * cells, :] = a.T
        at_ref[f * cells:(f + 1) * cells, blocks:] = int_ref[f]
        parts.append(jnp.concatenate(
            [at_ref[pl.ds(f * cells + x, zy, stride=E), :] for x in range(E)], axis=1))
    w = jnp.concatenate(parts, axis=0)
    hi = w.astype(jnp.bfloat16)
    rest = w - hi.astype(jnp.float32)
    mid = rest.astype(jnp.bfloat16)
    lo = (rest - mid.astype(jnp.float32)).astype(jnp.bfloat16)
    res = jnp.dot(jnp.concatenate([hi, mid, lo], axis=0), p_ref[...], preferred_element_type=jnp.float32)
    n = fields * zy
    out = (res[:n] + res[n:2 * n]) + res[2 * n:]
    width = o_ref.shape[3]
    count = o_ref.shape[2] // E
    for f in range(fields):
        for by in range(count):
            piece = out[f * zy:(f + 1) * zy, by * width:(by + 1) * width].reshape(E, E, width)
            o_ref[f, :, by * E:(by + 1) * E, :] = piece
            zt_ref[f, :, by * E:(by + 1) * E, :] = piece[E - 2:]
            zb_ref[f, :, by * E:(by + 1) * E, :] = piece[:2]
            if by == 0:
                yb_ref[f] = piece[:, :2, :]
            if by == count - 1:
                yt_ref[f] = piece[:, E - 2:, :]


def onehot_kernel(src_ref, p_ref):
    rows = p_ref.shape[0] // E
    lanes = src_ref.shape[1]
    row = lax.broadcasted_iota(jnp.int32, (rows, lanes), 0)
    lane = lax.broadcasted_iota(jnp.int32, (rows, lanes), 1)
    hit = row == src_ref[...]
    for x in range(E):
        sel = hit & (lane % E == x)
        p_ref[x * rows:(x + 1) * rows, :] = jnp.where(sel, 1.0, 0.0).astype(jnp.bfloat16)


def build_onehot(srcrow, rows):
    lanes = srcrow.shape[1]
    return pl.pallas_call(
        onehot_kernel,
        out_shape=jax.ShapeDtypeStruct((E * rows, lanes), jnp.bfloat16),
        interpret=INTERPRET,
    )(srcrow)


def assemble(arrived, interp, onehot):
    fields, cells, blocks = interp.shape
    return pl.pallas_call(
        assemble_kernel,
        out_shape=[
            jax.ShapeDtypeStruct((fields, E, BY * E, BX * E), jnp.float32),
            jax.ShapeDtypeStruct((fields, 2, BY * E, BX * E), jnp.float32),
            jax.ShapeDtypeStruct((fields, 2, BY * E, BX * E), jnp.float32),
            jax.ShapeDtypeStruct((fields, E, 2, BX * E), jnp.float32),
            jax.ShapeDtypeStruct((fields, E, 2, BX * E), jnp.float32),
        ],
        scratch_shapes=[pltpu.VMEM((fields * cells, 2 * blocks), jnp.float32)],
        interpret=INTERPRET,
    )(arrived, interp, onehot)


def kernel_minmod(left, right):
    rising = (left > 0) & (right > 0)
    falling = (left < 0) & (right < 0)
    return jnp.where(rising, jnp.minimum(left, right), jnp.where(falling, jnp.maximum(left, right), 0.0))


def face(below, cell, above):
    return cell + 0.5 * kernel_minmod(cell - below, above - cell)


def advance_kernel(c_ref, u_ref, zl_ref, zh_ref, yl_ref, yh_ref, o_ref, yp_ref, g_ref):
    f = pl.program_id(0)
    zn, yn, xn = u_ref.shape[1:]
    cz = c_ref[0, f]
    cy = c_ref[1, f]
    cx = c_ref[2, f]
    yp_ref[:, E - 2:E, :] = yl_ref[0]
    yp_ref[:, E:E + yn, :] = u_ref[0]
    yp_ref[:, E + yn:E + yn + 2, :] = yh_ref[0]
    span = g_ref.shape[0]
    lane = lax.broadcasted_iota(jnp.int32, (yn, xn), 1)

    def plane(j):
        if j < 2:
            return zl_ref[0, j]
        if j < zn + 2:
            return u_ref[0, j - 2]
        return zh_ref[0, j - zn - 2]

    g_prev = face(plane(0), plane(1), plane(2))
    for z in range(zn):
        u = plane(z + 2)
        g_next = face(plane(z + 1), u, plane(z + 3))
        tz = cz * (g_next - g_prev)
        g_prev = g_next
        g_ref[...] = face(yp_ref[z, E - 2:E - 2 + span, :], yp_ref[z, E - 1:E - 1 + span, :],
                          yp_ref[z, E:E + span, :])
        ty = cy * (g_ref[1:yn + 1, :] - g_ref[0:yn, :])
        lower1 = jnp.where(lane >= 1, pltpu.roll(u, 1, 1), 0.0)
        upper1 = jnp.where(lane < xn - 1, pltpu.roll(u, xn - 1, 1), 0.0)
        gx = face(lower1, u, upper1)
        gx_lo = jnp.where(lane >= 1, pltpu.roll(gx, 1, 1), 0.0)
        tx = cx * (gx - gx_lo)
        o_ref[0, z] = u - ((tz + ty) + tx)


def advance(courant, region, zlo, zhi, ylo, yhi):
    fields, zn, yn, xn = region.shape
    return pl.pallas_call(
        advance_kernel,
        grid=(fields,),
        in_specs=[
            pl.BlockSpec(memory_space=pltpu.SMEM),
            pl.BlockSpec((1, zn, yn, xn), lambda f: (f, 0, 0, 0)),
            pl.BlockSpec((1, 2, yn, xn), lambda f: (f, 0, 0, 0)),
            pl.BlockSpec((1, 2, yn, xn), lambda f: (f, 0, 0, 0)),
            pl.BlockSpec((1, zn, 2, xn), lambda f: (f, 0, 0, 0)),
            pl.BlockSpec((1, zn, 2, xn), lambda f: (f, 0, 0, 0)),
        ],
        out_specs=pl.BlockSpec((1, zn, yn, xn), lambda f: (f, 0, 0, 0)),
        out_shape=jax.ShapeDtypeStruct(region.shape, jnp.float32),
        scratch_shapes=[
            pltpu.VMEM((zn, yn + 2 * E, xn), jnp.float32),
            pltpu.VMEM((yn + E, xn), jnp.float32),
        ],
        compiler_params=pltpu.CompilerParams(dimension_semantics=("arbitrary",)),
        interpret=INTERPRET,
    )(courant, region, zlo, zhi, ylo, yhi)


def exchange(top, bottom, axis):
    count = lax.axis_size(axis)
    forward = [(i, i + 1) for i in range(count - 1)]
    backward = [(target, source) for source, target in forward]
    return lax.ppermute(top, axis, forward), lax.ppermute(bottom, axis, backward)


def local(old_fine, coarse_fine, old_owner, new_refine, parent_map, courant):
    slabs = lax.axis_size("slab")
    tiles = lax.axis_size("tile")
    myself = lax.axis_index("tile")
    blocks, fields, cells = old_fine.shape
    per_peer = blocks // tiles
    half = E // 2

    coarse_prev = lax.ppermute(coarse_fine, "slab", [(i, (i + 1) % slabs) for i in range(slabs)])

    owner = old_owner.reshape(-1)
    slot = jnp.arange(blocks, dtype=jnp.int32)
    same = owner[:, None] == owner[None, :]
    rank = jnp.sum((same & (slot[None, :] < slot[:, None])).astype(jnp.int32), axis=1)
    position = owner * per_peer + rank
    send_idx = jnp.sum(jnp.where(position[None, :] == slot[:, None], slot[None, :], 0), axis=1)
    outgoing = old_fine[send_idx].reshape(tiles, per_peer * fields * cells // 128, 128)
    arrived = lax.all_to_all(outgoing, "tile", split_axis=0, concat_axis=0, tiled=True)
    arrived = arrived.reshape(-1, 128)
    source = (2 * myself - owner) % tiles
    inverse = source * per_peer + rank

    parents = coarse_prev[parent_map.reshape(-1)]
    parents = parents.transpose(1, 2, 0).reshape(fields, half, half, half, blocks)
    interp = refine_block_kt(parents)

    flags = new_refine.reshape(-1)
    src = jnp.where(flags == 1, blocks + slot, inverse)
    onehot = build_onehot(jnp.repeat(src, E)[None, :], 2 * blocks)
    region, ztop, zbot, ytop, ybot = assemble(arrived, interp, onehot)

    zlo, zhi = exchange(ztop, zbot, "slab")
    ylo, yhi = exchange(ytop, ybot, "tile")
    return advance(courant, region, zlo, zhi, ylo, yhi)


def solution(mesh):
    in_specs = (
        P(("slab", "tile"), None, None),
        P(("slab", "tile"), None, None),
        P("slab", "tile", None),
        P("slab", "tile", None),
        P("slab", "tile", None),
        P(),
    )
    out_specs = P(None, "slab", "tile", None)
    return jax.shard_map(local, mesh=mesh, in_specs=in_specs, out_specs=out_specs, check_vma=False)
```

```python
import jax
import jax.numpy as jnp
from jax import lax
from jax.experimental import pallas as pl
from jax.experimental.pallas import tpu as pltpu
from jax.sharding import PartitionSpec as P

E = 8
BX = 16
BY = 4
INTERPRET = False


def slopes_kt(cells, axis):
    width = [(0, 0)] * cells.ndim
    width[axis] = (1, 1)
    padded = jnp.pad(cells, width, mode="edge")
    size = cells.shape[axis]
    below = lax.slice_in_dim(padded, 0, size, axis=axis)
    above = lax.slice_in_dim(padded, 2, size + 2, axis=axis)
    return kernel_minmod(cells - below, above - cells)


def refine_block_kt(cells):
    nd = cells.ndim
    slope_z = slopes_kt(cells, nd - 4)
    slope_y = slopes_kt(cells, nd - 3)
    slope_x = slopes_kt(cells, nd - 2)
    sigma = jnp.array([-0.25, 0.25], jnp.float32)

    def spread(value):
        return value[..., :, None, :, None, :, None, :]

    offset = (
        spread(slope_z) * sigma[:, None, None, None, None, None]
        + spread(slope_y) * sigma[:, None, None, None]
        + spread(slope_x) * sigma[:, None]
    )
    fine = spread(cells) + offset
    half = cells.shape[-2]
    return fine.reshape(cells.shape[:-4] + ((2 * half) ** 3, cells.shape[-1]))


def assemble_kernel(arr_ref, int_ref, p_ref, o_ref, zt_ref, zb_ref, yt_ref, yb_ref, at_ref):
    fields, cells, blocks = int_ref.shape
    stride = arr_ref.shape[0] // blocks
    quarters = cells // arr_ref.shape[1]
    zy = cells // E
    parts = []
    for f in range(fields):
        moved = jnp.concatenate(
            [arr_ref[pl.ds(f * quarters + q, blocks, stride=stride), :] for q in range(quarters)], axis=1)
        a = jnp.concatenate([moved, jnp.zeros_like(moved)], axis=0)
        at_ref[f * cells:(f + 1) * cells, :] = a.T
        at_ref[f * cells:(f + 1) * cells, blocks:] = int_ref[f]
        parts.append(jnp.concatenate(
            [at_ref[pl.ds(f * cells + x, zy, stride=E), :] for x in range(E)], axis=1))
    w = jnp.concatenate(parts, axis=0)
    hi = w.astype(jnp.bfloat16)
    rest = w - hi.astype(jnp.float32)
    mid = rest.astype(jnp.bfloat16)
    lo = (rest - mid.astype(jnp.float32)).astype(jnp.bfloat16)
    res = jnp.dot(jnp.concatenate([hi, mid, lo], axis=0), p_ref[...], preferred_element_type=jnp.float32)
    n = fields * zy
    out = (res[:n] + res[n:2 * n]) + res[2 * n:]
    width = o_ref.shape[3]
    count = o_ref.shape[2] // E
    for f in range(fields):
        for by in range(count):
            piece = out[f * zy:(f + 1) * zy, by * width:(by + 1) * width].reshape(E, E, width)
            o_ref[f, :, by * E:(by + 1) * E, :] = piece
            zt_ref[f, :, by * E:(by + 1) * E, :] = piece[E - 2:]
            zb_ref[f, :, by * E:(by + 1) * E, :] = piece[:2]
            if by == 0:
                yb_ref[f] = piece[:, :2, :]
            if by == count - 1:
                yt_ref[f] = piece[:, E - 2:, :]


def onehot_kernel(src_ref, p_ref):
    rows = p_ref.shape[0] // E
    lanes = src_ref.shape[1]
    row = lax.broadcasted_iota(jnp.int32, (rows, lanes), 0)
    lane = lax.broadcasted_iota(jnp.int32, (rows, lanes), 1)
    hit = row == src_ref[...]
    for x in range(E):
        sel = hit & (lane % E == x)
        p_ref[x * rows:(x + 1) * rows, :] = jnp.where(sel, 1.0, 0.0).astype(jnp.bfloat16)


def build_onehot(srcrow, rows):
    lanes = srcrow.shape[1]
    return pl.pallas_call(
        onehot_kernel,
        out_shape=jax.ShapeDtypeStruct((E * rows, lanes), jnp.bfloat16),
        interpret=INTERPRET,
    )(srcrow)


def assemble(arrived, interp, onehot):
    fields, cells, blocks = interp.shape
    return pl.pallas_call(
        assemble_kernel,
        out_shape=[
            jax.ShapeDtypeStruct((fields, E, BY * E, BX * E), jnp.float32),
            jax.ShapeDtypeStruct((fields, 2, BY * E, BX * E), jnp.float32),
            jax.ShapeDtypeStruct((fields, 2, BY * E, BX * E), jnp.float32),
            jax.ShapeDtypeStruct((fields, E, 2, BX * E), jnp.float32),
            jax.ShapeDtypeStruct((fields, E, 2, BX * E), jnp.float32),
        ],
        scratch_shapes=[pltpu.VMEM((fields * cells, 2 * blocks), jnp.float32)],
        interpret=INTERPRET,
    )(arrived, interp, onehot)


def kernel_minmod(left, right):
    return jnp.maximum(jnp.minimum(left, right), jnp.minimum(0.0, jnp.maximum(left, right)))


def face(below, cell, above):
    return cell + 0.5 * kernel_minmod(cell - below, above - cell)


def advance_kernel(c_ref, u_ref, zl_ref, zh_ref, yl_ref, yh_ref, o_ref, yp_ref, g_ref):
    f = pl.program_id(0)
    zn, yn, xn = u_ref.shape[1:]
    cz = c_ref[0, f]
    cy = c_ref[1, f]
    cx = c_ref[2, f]
    yp_ref[:, E - 2:E, :] = yl_ref[0]
    yp_ref[:, E:E + yn, :] = u_ref[0]
    yp_ref[:, E + yn:E + yn + 2, :] = yh_ref[0]
    span = g_ref.shape[0]
    lane = lax.broadcasted_iota(jnp.int32, (yn, xn), 1)

    def plane(j):
        if j < 2:
            return zl_ref[0, j]
        if j < zn + 2:
            return u_ref[0, j - 2]
        return zh_ref[0, j - zn - 2]

    g_prev = face(plane(0), plane(1), plane(2))
    for z in range(zn):
        u = plane(z + 2)
        g_next = face(plane(z + 1), u, plane(z + 3))
        tz = cz * (g_next - g_prev)
        g_prev = g_next
        g_ref[...] = face(yp_ref[z, E - 2:E - 2 + span, :], yp_ref[z, E - 1:E - 1 + span, :],
                          yp_ref[z, E:E + span, :])
        ty = cy * (g_ref[1:yn + 1, :] - g_ref[0:yn, :])
        lower1 = jnp.where(lane >= 1, pltpu.roll(u, 1, 1), 0.0)
        upper1 = jnp.where(lane < xn - 1, pltpu.roll(u, xn - 1, 1), 0.0)
        gx = face(lower1, u, upper1)
        gx_lo = jnp.where(lane >= 1, pltpu.roll(gx, 1, 1), 0.0)
        tx = cx * (gx - gx_lo)
        o_ref[0, z] = u - ((tz + ty) + tx)


def advance(courant, region, zlo, zhi, ylo, yhi):
    fields, zn, yn, xn = region.shape
    return pl.pallas_call(
        advance_kernel,
        grid=(fields,),
        in_specs=[
            pl.BlockSpec(memory_space=pltpu.SMEM),
            pl.BlockSpec((1, zn, yn, xn), lambda f: (f, 0, 0, 0)),
            pl.BlockSpec((1, 2, yn, xn), lambda f: (f, 0, 0, 0)),
            pl.BlockSpec((1, 2, yn, xn), lambda f: (f, 0, 0, 0)),
            pl.BlockSpec((1, zn, 2, xn), lambda f: (f, 0, 0, 0)),
            pl.BlockSpec((1, zn, 2, xn), lambda f: (f, 0, 0, 0)),
        ],
        out_specs=pl.BlockSpec((1, zn, yn, xn), lambda f: (f, 0, 0, 0)),
        out_shape=jax.ShapeDtypeStruct(region.shape, jnp.float32),
        scratch_shapes=[
            pltpu.VMEM((zn, yn + 2 * E, xn), jnp.float32),
            pltpu.VMEM((yn + E, xn), jnp.float32),
        ],
        compiler_params=pltpu.CompilerParams(dimension_semantics=("arbitrary",)),
        interpret=INTERPRET,
    )(courant, region, zlo, zhi, ylo, yhi)


def exchange(top, bottom, axis):
    count = lax.axis_size(axis)
    forward = [(i, i + 1) for i in range(count - 1)]
    backward = [(target, source) for source, target in forward]
    return lax.ppermute(top, axis, forward), lax.ppermute(bottom, axis, backward)


def local(old_fine, coarse_fine, old_owner, new_refine, parent_map, courant):
    slabs = lax.axis_size("slab")
    tiles = lax.axis_size("tile")
    myself = lax.axis_index("tile")
    blocks, fields, cells = old_fine.shape
    per_peer = blocks // tiles
    half = E // 2

    coarse_prev = lax.ppermute(coarse_fine, "slab", [(i, (i + 1) % slabs) for i in range(slabs)])

    owner = old_owner.reshape(-1)
    slot = jnp.arange(blocks, dtype=jnp.int32)
    same = owner[:, None] == owner[None, :]
    rank = jnp.sum((same & (slot[None, :] < slot[:, None])).astype(jnp.int32), axis=1)
    position = owner * per_peer + rank
    send_idx = jnp.sum(jnp.where(position[None, :] == slot[:, None], slot[None, :], 0), axis=1)
    outgoing = old_fine[send_idx].reshape(tiles, per_peer * fields * cells // 128, 128)
    arrived = lax.all_to_all(outgoing, "tile", split_axis=0, concat_axis=0, tiled=True)
    arrived = arrived.reshape(-1, 128)
    source = (2 * myself - owner) % tiles
    inverse = source * per_peer + rank

    parents = coarse_prev[parent_map.reshape(-1)]
    parents = parents.transpose(1, 2, 0).reshape(fields, half, half, half, blocks)
    interp = refine_block_kt(parents)

    flags = new_refine.reshape(-1)
    src = jnp.where(flags == 1, blocks + slot, inverse)
    onehot = build_onehot(jnp.repeat(src, E)[None, :], 2 * blocks)
    region, ztop, zbot, ytop, ybot = assemble(arrived, interp, onehot)

    zlo, zhi = exchange(ztop, zbot, "slab")
    ylo, yhi = exchange(ytop, ybot, "tile")
    return advance(courant, region, zlo, zhi, ylo, yhi)


def solution(mesh):
    in_specs = (
        P(("slab", "tile"), None, None),
        P(("slab", "tile"), None, None),
        P("slab", "tile", None),
        P("slab", "tile", None),
        P("slab", "tile", None),
        P(),
    )
    out_specs = P(None, "slab", "tile", None)
    return jax.shard_map(local, mesh=mesh, in_specs=in_specs, out_specs=out_specs, check_vma=False)
```

```python
import jax
import jax.numpy as jnp
from jax import lax
from jax.experimental import pallas as pl
from jax.experimental.pallas import tpu as pltpu
from jax.sharding import PartitionSpec as P

E = 8
BX = 16
BY = 4
INTERPRET = False


def slopes_kt(cells, axis):
    width = [(0, 0)] * cells.ndim
    width[axis] = (1, 1)
    padded = jnp.pad(cells, width, mode="edge")
    size = cells.shape[axis]
    below = lax.slice_in_dim(padded, 0, size, axis=axis)
    above = lax.slice_in_dim(padded, 2, size + 2, axis=axis)
    return kernel_minmod(cells - below, above - cells)


def refine_block_kt(cells):
    nd = cells.ndim
    slope_z = slopes_kt(cells, nd - 4)
    slope_y = slopes_kt(cells, nd - 3)
    slope_x = slopes_kt(cells, nd - 2)
    sigma = jnp.array([-0.25, 0.25], jnp.float32)

    def spread(value):
        return value[..., :, None, :, None, :, None, :]

    offset = (
        spread(slope_z) * sigma[:, None, None, None, None, None]
        + spread(slope_y) * sigma[:, None, None, None]
        + spread(slope_x) * sigma[:, None]
    )
    fine = spread(cells) + offset
    half = cells.shape[-2]
    return fine.reshape(cells.shape[:-4] + ((2 * half) ** 3, cells.shape[-1]))


def assemble_kernel(arr_ref, int_ref, p_ref, o_ref, zt_ref, zb_ref, yt_ref, yb_ref, at_ref):
    fields, cells, blocks = int_ref.shape
    stride = arr_ref.shape[0] // blocks
    quarters = cells // arr_ref.shape[1]
    zy = cells // E
    parts = []
    for f in range(fields):
        moved = jnp.concatenate(
            [arr_ref[pl.ds(f * quarters + q, blocks, stride=stride), :] for q in range(quarters)], axis=1)
        a = jnp.concatenate([moved, jnp.zeros_like(moved)], axis=0)
        at_ref[f * cells:(f + 1) * cells, :] = a.T
        at_ref[f * cells:(f + 1) * cells, blocks:] = int_ref[f]
        parts.append(jnp.concatenate(
            [at_ref[pl.ds(f * cells + x, zy, stride=E), :] for x in range(E)], axis=1))
    w = jnp.concatenate(parts, axis=0)
    hi = w.astype(jnp.bfloat16)
    rest = w - hi.astype(jnp.float32)
    mid = rest.astype(jnp.bfloat16)
    lo = (rest - mid.astype(jnp.float32)).astype(jnp.bfloat16)
    res = jnp.dot(jnp.concatenate([hi, mid, lo], axis=0), p_ref[...], preferred_element_type=jnp.float32)
    n = fields * zy
    out = (res[:n] + res[n:2 * n]) + res[2 * n:]
    width = o_ref.shape[3]
    count = o_ref.shape[2] // E
    for f in range(fields):
        for by in range(count):
            piece = out[f * zy:(f + 1) * zy, by * width:(by + 1) * width].reshape(E, E, width)
            o_ref[f, :, by * E:(by + 1) * E, :] = piece
            zt_ref[f, :, by * E:(by + 1) * E, :] = piece[E - 2:]
            zb_ref[f, :, by * E:(by + 1) * E, :] = piece[:2]
            if by == 0:
                yb_ref[f] = piece[:, :2, :]
            if by == count - 1:
                yt_ref[f] = piece[:, E - 2:, :]


def onehot_kernel(src_ref, p_ref):
    rows = p_ref.shape[0] // E
    lanes = src_ref.shape[1]
    row = lax.broadcasted_iota(jnp.int32, (rows, lanes), 0)
    lane = lax.broadcasted_iota(jnp.int32, (rows, lanes), 1)
    hit = row == src_ref[...]
    for x in range(E):
        sel = hit & (lane % E == x)
        p_ref[x * rows:(x + 1) * rows, :] = jnp.where(sel, 1.0, 0.0).astype(jnp.bfloat16)


def build_onehot(srcrow, rows):
    lanes = srcrow.shape[1]
    return pl.pallas_call(
        onehot_kernel,
        out_shape=jax.ShapeDtypeStruct((E * rows, lanes), jnp.bfloat16),
        interpret=INTERPRET,
    )(srcrow)


def assemble(arrived, interp, onehot):
    fields, cells, blocks = interp.shape
    return pl.pallas_call(
        assemble_kernel,
        out_shape=[
            jax.ShapeDtypeStruct((fields, E, BY * E, BX * E), jnp.float32),
            jax.ShapeDtypeStruct((fields, 2, BY * E, BX * E), jnp.float32),
            jax.ShapeDtypeStruct((fields, 2, BY * E, BX * E), jnp.float32),
            jax.ShapeDtypeStruct((fields, E, 2, BX * E), jnp.float32),
            jax.ShapeDtypeStruct((fields, E, 2, BX * E), jnp.float32),
        ],
        scratch_shapes=[pltpu.VMEM((fields * cells, 2 * blocks), jnp.float32)],
        interpret=INTERPRET,
    )(arrived, interp, onehot)


def kernel_minmod(left, right):
    return jnp.maximum(jnp.minimum(left, right), jnp.minimum(0.0, jnp.maximum(left, right)))


def face(below, cell, above):
    return cell + 0.5 * kernel_minmod(cell - below, above - cell)


def advance_kernel(c_ref, u_ref, zl_ref, zh_ref, yl_ref, yh_ref, o_ref, yp_ref, g_ref):
    fields, zn, yn, xn = u_ref.shape
    span = g_ref.shape[0]
    lane = lax.broadcasted_iota(jnp.int32, (yn, xn), 1)
    for f in range(fields):
        cz = c_ref[0, f]
        cy = c_ref[1, f]
        cx = c_ref[2, f]
        yp_ref[:, E - 2:E, :] = yl_ref[f]
        yp_ref[:, E:E + yn, :] = u_ref[f]
        yp_ref[:, E + yn:E + yn + 2, :] = yh_ref[f]

        def plane(j):
            if j < 2:
                return zl_ref[f, j]
            if j < zn + 2:
                return u_ref[f, j - 2]
            return zh_ref[f, j - zn - 2]

        g_prev = face(plane(0), plane(1), plane(2))
        for z in range(zn):
            u = plane(z + 2)
            g_next = face(plane(z + 1), u, plane(z + 3))
            tz = cz * (g_next - g_prev)
            g_prev = g_next
            g_ref[...] = face(yp_ref[z, E - 2:E - 2 + span, :], yp_ref[z, E - 1:E - 1 + span, :],
                              yp_ref[z, E:E + span, :])
            ty = cy * (g_ref[1:yn + 1, :] - g_ref[0:yn, :])
            lower1 = jnp.where(lane >= 1, pltpu.roll(u, 1, 1), 0.0)
            upper1 = jnp.where(lane < xn - 1, pltpu.roll(u, xn - 1, 1), 0.0)
            gx = face(lower1, u, upper1)
            gx_lo = jnp.where(lane >= 1, pltpu.roll(gx, 1, 1), 0.0)
            tx = cx * (gx - gx_lo)
            o_ref[f, z] = u - ((tz + ty) + tx)


def advance(courant, region, zlo, zhi, ylo, yhi):
    _, zn, yn, xn = region.shape
    vmem = pl.BlockSpec(memory_space=pltpu.VMEM)
    return pl.pallas_call(
        advance_kernel,
        in_specs=[pl.BlockSpec(memory_space=pltpu.SMEM), vmem, vmem, vmem, vmem, vmem],
        out_specs=vmem,
        out_shape=jax.ShapeDtypeStruct(region.shape, jnp.float32),
        scratch_shapes=[
            pltpu.VMEM((zn, yn + 2 * E, xn), jnp.float32),
            pltpu.VMEM((yn + E, xn), jnp.float32),
        ],
        interpret=INTERPRET,
    )(courant, region, zlo, zhi, ylo, yhi)


def exchange(top, bottom, axis):
    count = lax.axis_size(axis)
    forward = [(i, i + 1) for i in range(count - 1)]
    backward = [(target, source) for source, target in forward]
    return lax.ppermute(top, axis, forward), lax.ppermute(bottom, axis, backward)


def local(old_fine, coarse_fine, old_owner, new_refine, parent_map, courant):
    slabs = lax.axis_size("slab")
    tiles = lax.axis_size("tile")
    myself = lax.axis_index("tile")
    blocks, fields, cells = old_fine.shape
    per_peer = blocks // tiles
    half = E // 2

    coarse_prev = lax.ppermute(coarse_fine, "slab", [(i, (i + 1) % slabs) for i in range(slabs)])

    owner = old_owner.reshape(-1)
    slot = jnp.arange(blocks, dtype=jnp.int32)
    same = owner[:, None] == owner[None, :]
    rank = jnp.sum((same & (slot[None, :] < slot[:, None])).astype(jnp.int32), axis=1)
    position = owner * per_peer + rank
    send_idx = jnp.sum(jnp.where(position[None, :] == slot[:, None], slot[None, :], 0), axis=1)
    outgoing = old_fine[send_idx].reshape(tiles, per_peer * fields * cells // 128, 128)
    arrived = lax.all_to_all(outgoing, "tile", split_axis=0, concat_axis=0, tiled=True)
    arrived = arrived.reshape(-1, 128)
    source = (2 * myself - owner) % tiles
    inverse = source * per_peer + rank

    parents = coarse_prev[parent_map.reshape(-1)]
    parents = parents.transpose(1, 2, 0).reshape(fields, half, half, half, blocks)
    interp = refine_block_kt(parents)

    flags = new_refine.reshape(-1)
    src = jnp.where(flags == 1, blocks + slot, inverse)
    onehot = build_onehot(jnp.repeat(src, E)[None, :], 2 * blocks)
    region, ztop, zbot, ytop, ybot = assemble(arrived, interp, onehot)

    zlo, zhi = exchange(ztop, zbot, "slab")
    ylo, yhi = exchange(ytop, ybot, "tile")
    return advance(courant, region, zlo, zhi, ylo, yhi)


def solution(mesh):
    in_specs = (
        P(("slab", "tile"), None, None),
        P(("slab", "tile"), None, None),
        P("slab", "tile", None),
        P("slab", "tile", None),
        P("slab", "tile", None),
        P(),
    )
    out_specs = P(None, "slab", "tile", None)
    return jax.shard_map(local, mesh=mesh, in_specs=in_specs, out_specs=out_specs, check_vma=False)
```

```python
import jax
import jax.numpy as jnp
from jax import lax
from jax.experimental import pallas as pl
from jax.experimental.pallas import tpu as pltpu
from jax.sharding import PartitionSpec as P

E = 8
BX = 16
BY = 4
INTERPRET = False


def slopes_kt(cells, axis):
    width = [(0, 0)] * cells.ndim
    width[axis] = (1, 1)
    padded = jnp.pad(cells, width, mode="edge")
    size = cells.shape[axis]
    below = lax.slice_in_dim(padded, 0, size, axis=axis)
    above = lax.slice_in_dim(padded, 2, size + 2, axis=axis)
    return kernel_minmod(cells - below, above - cells)


def refine_block_kt(cells):
    nd = cells.ndim
    slope_z = slopes_kt(cells, nd - 4)
    slope_y = slopes_kt(cells, nd - 3)
    slope_x = slopes_kt(cells, nd - 2)
    sigma = jnp.array([-0.25, 0.25], jnp.float32)

    def spread(value):
        return value[..., :, None, :, None, :, None, :]

    offset = (
        spread(slope_z) * sigma[:, None, None, None, None, None]
        + spread(slope_y) * sigma[:, None, None, None]
        + spread(slope_x) * sigma[:, None]
    )
    fine = spread(cells) + offset
    half = cells.shape[-2]
    return fine.reshape(cells.shape[:-4] + ((2 * half) ** 3, cells.shape[-1]))


def assemble_kernel(arr_ref, int_ref, p_ref, o_ref, zt_ref, zb_ref, yt_ref, yb_ref, at_ref):
    fields, cells, blocks = int_ref.shape
    stride = arr_ref.shape[0] // blocks
    quarters = cells // arr_ref.shape[1]
    zy = cells // E
    parts = []
    for f in range(fields):
        moved = jnp.concatenate(
            [arr_ref[pl.ds(f * quarters + q, blocks, stride=stride), :] for q in range(quarters)], axis=1)
        a = jnp.concatenate([moved, jnp.zeros_like(moved)], axis=0)
        at_ref[f * cells:(f + 1) * cells, :] = a.T
        at_ref[f * cells:(f + 1) * cells, blocks:] = int_ref[f]
        parts.append(jnp.concatenate(
            [at_ref[pl.ds(f * cells + x, zy, stride=E), :] for x in range(E)], axis=1))
    w = jnp.concatenate(parts, axis=0)
    hi = w.astype(jnp.bfloat16)
    rest = w - hi.astype(jnp.float32)
    mid = rest.astype(jnp.bfloat16)
    lo = (rest - mid.astype(jnp.float32)).astype(jnp.bfloat16)
    res = jnp.dot(jnp.concatenate([hi, mid, lo], axis=0), p_ref[...], preferred_element_type=jnp.float32)
    n = fields * zy
    out = (res[:n] + res[n:2 * n]) + res[2 * n:]
    width = o_ref.shape[3]
    count = o_ref.shape[2] // E
    for f in range(fields):
        for by in range(count):
            piece = out[f * zy:(f + 1) * zy, by * width:(by + 1) * width].reshape(E, E, width)
            o_ref[f, :, by * E:(by + 1) * E, :] = piece
            zt_ref[f, :, by * E:(by + 1) * E, :] = piece[E - 2:]
            zb_ref[f, :, by * E:(by + 1) * E, :] = piece[:2]
            if by == 0:
                yb_ref[f] = piece[:, :2, :]
            if by == count - 1:
                yt_ref[f] = piece[:, E - 2:, :]


def onehot_kernel(src_ref, p_ref):
    rows = p_ref.shape[0] // E
    lanes = src_ref.shape[1]
    row = lax.broadcasted_iota(jnp.int32, (rows, lanes), 0)
    lane = lax.broadcasted_iota(jnp.int32, (rows, lanes), 1)
    hit = row == src_ref[...]
    for x in range(E):
        sel = hit & (lane % E == x)
        p_ref[x * rows:(x + 1) * rows, :] = jnp.where(sel, 1.0, 0.0).astype(jnp.bfloat16)


def build_onehot(srcrow, rows):
    lanes = srcrow.shape[1]
    return pl.pallas_call(
        onehot_kernel,
        out_shape=jax.ShapeDtypeStruct((E * rows, lanes), jnp.bfloat16),
        interpret=INTERPRET,
    )(srcrow)


def assemble(arrived, interp, onehot):
    fields, cells, blocks = interp.shape
    return pl.pallas_call(
        assemble_kernel,
        out_shape=[
            jax.ShapeDtypeStruct((fields, E, BY * E, BX * E), jnp.float32),
            jax.ShapeDtypeStruct((fields, 2, BY * E, BX * E), jnp.float32),
            jax.ShapeDtypeStruct((fields, 2, BY * E, BX * E), jnp.float32),
            jax.ShapeDtypeStruct((fields, E, 2, BX * E), jnp.float32),
            jax.ShapeDtypeStruct((fields, E, 2, BX * E), jnp.float32),
        ],
        scratch_shapes=[pltpu.VMEM((fields * cells, 2 * blocks), jnp.float32)],
        interpret=INTERPRET,
    )(arrived, interp, onehot)


def kernel_minmod(left, right):
    return jnp.maximum(jnp.minimum(left, right), jnp.minimum(0.0, jnp.maximum(left, right)))


def face(below, cell, above):
    return cell + 0.5 * kernel_minmod(cell - below, above - cell)


def advance_kernel(c_ref, u_ref, zl_ref, zh_ref, yl_ref, yh_ref, o_ref):
    fields, zn, yn, xn = u_ref.shape
    lane = lax.broadcasted_iota(jnp.int32, (yn, xn), 1)
    row = lax.broadcasted_iota(jnp.int32, (yn, xn), 0)
    for f in range(fields):
        cz = c_ref[0, f]
        cy = c_ref[1, f]
        cx = c_ref[2, f]

        def plane(j):
            if j < 2:
                return zl_ref[f, j]
            if j < zn + 2:
                return u_ref[f, j - 2]
            return zh_ref[f, j - zn - 2]

        g_prev = face(plane(0), plane(1), plane(2))
        for z in range(zn):
            u = plane(z + 2)
            g_next = face(plane(z + 1), u, plane(z + 3))
            tz = cz * (g_next - g_prev)
            g_prev = g_next
            ylo = yl_ref[f, z]
            yhi = yh_ref[f, z]
            below = jnp.where(row == 0, ylo[1:2], pltpu.roll(u, 1, 0))
            above = jnp.where(row == yn - 1, yhi[0:1], pltpu.roll(u, yn - 1, 0))
            gy = face(below, u, above)
            gy_first = face(ylo[0:1], ylo[1:2], u[0:1])
            gy_lo = jnp.where(row == 0, gy_first, pltpu.roll(gy, 1, 0))
            ty = cy * (gy - gy_lo)
            lower1 = jnp.where(lane >= 1, pltpu.roll(u, 1, 1), 0.0)
            upper1 = jnp.where(lane < xn - 1, pltpu.roll(u, xn - 1, 1), 0.0)
            gx = face(lower1, u, upper1)
            gx_lo = jnp.where(lane >= 1, pltpu.roll(gx, 1, 1), 0.0)
            tx = cx * (gx - gx_lo)
            o_ref[f, z] = u - ((tz + ty) + tx)


def advance(courant, region, zlo, zhi, ylo, yhi):
    vmem = pl.BlockSpec(memory_space=pltpu.VMEM)
    return pl.pallas_call(
        advance_kernel,
        in_specs=[pl.BlockSpec(memory_space=pltpu.SMEM), vmem, vmem, vmem, vmem, vmem],
        out_specs=vmem,
        out_shape=jax.ShapeDtypeStruct(region.shape, jnp.float32),
        interpret=INTERPRET,
    )(courant, region, zlo, zhi, ylo, yhi)


def exchange(top, bottom, axis):
    count = lax.axis_size(axis)
    forward = [(i, i + 1) for i in range(count - 1)]
    backward = [(target, source) for source, target in forward]
    return lax.ppermute(top, axis, forward), lax.ppermute(bottom, axis, backward)


def local(old_fine, coarse_fine, old_owner, new_refine, parent_map, courant):
    slabs = lax.axis_size("slab")
    tiles = lax.axis_size("tile")
    myself = lax.axis_index("tile")
    blocks, fields, cells = old_fine.shape
    per_peer = blocks // tiles
    half = E // 2

    coarse_prev = lax.ppermute(coarse_fine, "slab", [(i, (i + 1) % slabs) for i in range(slabs)])

    owner = old_owner.reshape(-1)
    slot = jnp.arange(blocks, dtype=jnp.int32)
    same = owner[:, None] == owner[None, :]
    rank = jnp.sum((same & (slot[None, :] < slot[:, None])).astype(jnp.int32), axis=1)
    position = owner * per_peer + rank
    send_idx = jnp.sum(jnp.where(position[None, :] == slot[:, None], slot[None, :], 0), axis=1)
    outgoing = old_fine[send_idx].reshape(tiles, per_peer * fields * cells // 128, 128)
    arrived = lax.all_to_all(outgoing, "tile", split_axis=0, concat_axis=0, tiled=True)
    arrived = arrived.reshape(-1, 128)
    source = (2 * myself - owner) % tiles
    inverse = source * per_peer + rank

    parents = coarse_prev[parent_map.reshape(-1)]
    parents = parents.transpose(1, 2, 0).reshape(fields, half, half, half, blocks)
    interp = refine_block_kt(parents)

    flags = new_refine.reshape(-1)
    src = jnp.where(flags == 1, blocks + slot, inverse)
    onehot = build_onehot(jnp.repeat(src, E)[None, :], 2 * blocks)
    region, ztop, zbot, ytop, ybot = assemble(arrived, interp, onehot)

    zlo, zhi = exchange(ztop, zbot, "slab")
    ylo, yhi = exchange(ytop, ybot, "tile")
    return advance(courant, region, zlo, zhi, ylo, yhi)


def solution(mesh):
    in_specs = (
        P(("slab", "tile"), None, None),
        P(("slab", "tile"), None, None),
        P("slab", "tile", None),
        P("slab", "tile", None),
        P("slab", "tile", None),
        P(),
    )
    out_specs = P(None, "slab", "tile", None)
    return jax.shard_map(local, mesh=mesh, in_specs=in_specs, out_specs=out_specs, check_vma=False)
```

```python
import jax
import jax.numpy as jnp
from jax import lax
from jax.experimental import pallas as pl
from jax.experimental.pallas import tpu as pltpu
from jax.sharding import PartitionSpec as P

E = 8
BX = 16
BY = 4
INTERPRET = False


def slopes_kt(cells, axis):
    width = [(0, 0)] * cells.ndim
    width[axis] = (1, 1)
    padded = jnp.pad(cells, width, mode="edge")
    size = cells.shape[axis]
    below = lax.slice_in_dim(padded, 0, size, axis=axis)
    above = lax.slice_in_dim(padded, 2, size + 2, axis=axis)
    return kernel_minmod(cells - below, above - cells)


def refine_block_kt(cells):
    nd = cells.ndim
    slope_z = slopes_kt(cells, nd - 4)
    slope_y = slopes_kt(cells, nd - 3)
    slope_x = slopes_kt(cells, nd - 2)
    sigma = jnp.array([-0.25, 0.25], jnp.float32)

    def spread(value):
        return value[..., :, None, :, None, :, None, :]

    offset = (
        spread(slope_z) * sigma[:, None, None, None, None, None]
        + spread(slope_y) * sigma[:, None, None, None]
        + spread(slope_x) * sigma[:, None]
    )
    fine = spread(cells) + offset
    half = cells.shape[-2]
    return fine.reshape(cells.shape[:-4] + ((2 * half) ** 3, cells.shape[-1]))


def assemble_kernel(arr_ref, int_ref, p_ref, o_ref, zt_ref, zb_ref, yt_ref, yb_ref, at_ref):
    fields, cells, blocks = int_ref.shape
    stride = arr_ref.shape[0] // blocks
    quarters = cells // arr_ref.shape[1]
    zy = cells // E
    parts = []
    for f in range(fields):
        moved = jnp.concatenate(
            [arr_ref[pl.ds(f * quarters + q, blocks, stride=stride), :] for q in range(quarters)], axis=1)
        a = jnp.concatenate([moved, jnp.zeros_like(moved)], axis=0)
        at_ref[f * cells:(f + 1) * cells, :] = a.T
        at_ref[f * cells:(f + 1) * cells, blocks:] = int_ref[f]
        parts.append(jnp.concatenate(
            [at_ref[pl.ds(f * cells + x, zy, stride=E), :] for x in range(E)], axis=1))
    w = jnp.concatenate(parts, axis=0)
    hi = w.astype(jnp.bfloat16)
    rest = w - hi.astype(jnp.float32)
    mid = rest.astype(jnp.bfloat16)
    lo = (rest - mid.astype(jnp.float32)).astype(jnp.bfloat16)
    res = jnp.dot(jnp.concatenate([hi, mid, lo], axis=0), p_ref[...], preferred_element_type=jnp.float32)
    n = fields * zy
    out = (res[:n] + res[n:2 * n]) + res[2 * n:]
    width = o_ref.shape[3]
    count = o_ref.shape[2] // E
    for f in range(fields):
        for by in range(count):
            piece = out[f * zy:(f + 1) * zy, by * width:(by + 1) * width].reshape(E, E, width)
            o_ref[f, :, by * E:(by + 1) * E, :] = piece
            zt_ref[f, :, by * E:(by + 1) * E, :] = piece[E - 2:]
            zb_ref[f, :, by * E:(by + 1) * E, :] = piece[:2]
            if by == 0:
                yb_ref[f] = piece[:, :2, :]
            if by == count - 1:
                yt_ref[f] = piece[:, E - 2:, :]


def onehot_kernel(src_ref, p_ref):
    rows = p_ref.shape[0] // E
    lanes = src_ref.shape[1]
    row = lax.broadcasted_iota(jnp.int32, (rows, lanes), 0)
    lane = lax.broadcasted_iota(jnp.int32, (rows, lanes), 1)
    hit = row == src_ref[...]
    for x in range(E):
        sel = hit & (lane % E == x)
        p_ref[x * rows:(x + 1) * rows, :] = jnp.where(sel, 1.0, 0.0).astype(jnp.bfloat16)


def build_onehot(srcrow, rows):
    lanes = srcrow.shape[1]
    return pl.pallas_call(
        onehot_kernel,
        out_shape=jax.ShapeDtypeStruct((E * rows, lanes), jnp.bfloat16),
        interpret=INTERPRET,
    )(srcrow)


def assemble(arrived, interp, onehot):
    fields, cells, blocks = interp.shape
    return pl.pallas_call(
        assemble_kernel,
        out_shape=[
            jax.ShapeDtypeStruct((fields, E, BY * E, BX * E), jnp.float32),
            jax.ShapeDtypeStruct((fields, 2, BY * E, BX * E), jnp.float32),
            jax.ShapeDtypeStruct((fields, 2, BY * E, BX * E), jnp.float32),
            jax.ShapeDtypeStruct((fields, E, 2, BX * E), jnp.float32),
            jax.ShapeDtypeStruct((fields, E, 2, BX * E), jnp.float32),
        ],
        scratch_shapes=[pltpu.VMEM((fields * cells, 2 * blocks), jnp.float32)],
        interpret=INTERPRET,
    )(arrived, interp, onehot)


def kernel_minmod(left, right):
    return jnp.maximum(jnp.minimum(left, right), jnp.minimum(0.0, jnp.maximum(left, right)))


def face(below, cell, above):
    return cell + 0.5 * kernel_minmod(cell - below, above - cell)


def xterm_kernel(c_ref, u_ref, o_ref):
    fields, zn, yn, xn = u_ref.shape
    lane = lax.broadcasted_iota(jnp.int32, (yn, xn), 1)
    for f in range(fields):
        cx = c_ref[2, f]
        for z in range(zn):
            u = u_ref[f, z]
            lower1 = jnp.where(lane >= 1, pltpu.roll(u, 1, 1), 0.0)
            upper1 = jnp.where(lane < xn - 1, pltpu.roll(u, xn - 1, 1), 0.0)
            gx = face(lower1, u, upper1)
            gx_lo = jnp.where(lane >= 1, pltpu.roll(gx, 1, 1), 0.0)
            o_ref[f, z] = cx * (gx - gx_lo)


def xterm(courant, region):
    vmem = pl.BlockSpec(memory_space=pltpu.VMEM)
    return pl.pallas_call(
        xterm_kernel,
        in_specs=[pl.BlockSpec(memory_space=pltpu.SMEM), vmem],
        out_specs=vmem,
        out_shape=jax.ShapeDtypeStruct(region.shape, jnp.float32),
        interpret=INTERPRET,
    )(courant, region)


def advance_kernel(c_ref, u_ref, zl_ref, zh_ref, yl_ref, yh_ref, tx_ref, o_ref):
    fields, zn, yn, xn = u_ref.shape
    lane = lax.broadcasted_iota(jnp.int32, (yn, xn), 1)
    row = lax.broadcasted_iota(jnp.int32, (yn, xn), 0)
    for f in range(fields):
        cz = c_ref[0, f]
        cy = c_ref[1, f]

        def plane(j):
            if j < 2:
                return zl_ref[f, j]
            if j < zn + 2:
                return u_ref[f, j - 2]
            return zh_ref[f, j - zn - 2]

        g_prev = face(plane(0), plane(1), plane(2))
        for z in range(zn):
            u = plane(z + 2)
            g_next = face(plane(z + 1), u, plane(z + 3))
            tz = cz * (g_next - g_prev)
            g_prev = g_next
            ylo = yl_ref[f, z]
            yhi = yh_ref[f, z]
            below = jnp.where(row == 0, ylo[1:2], pltpu.roll(u, 1, 0))
            above = jnp.where(row == yn - 1, yhi[0:1], pltpu.roll(u, yn - 1, 0))
            gy = face(below, u, above)
            gy_first = face(ylo[0:1], ylo[1:2], u[0:1])
            gy_lo = jnp.where(row == 0, gy_first, pltpu.roll(gy, 1, 0))
            ty = cy * (gy - gy_lo)
            o_ref[f, z] = u - ((tz + ty) + tx_ref[f, z])


def advance(courant, region, zlo, zhi, ylo, yhi, tx):
    vmem = pl.BlockSpec(memory_space=pltpu.VMEM)
    return pl.pallas_call(
        advance_kernel,
        in_specs=[pl.BlockSpec(memory_space=pltpu.SMEM), vmem, vmem, vmem, vmem, vmem, vmem],
        out_specs=vmem,
        out_shape=jax.ShapeDtypeStruct(region.shape, jnp.float32),
        interpret=INTERPRET,
    )(courant, region, zlo, zhi, ylo, yhi, tx)


def exchange(top, bottom, axis):
    count = lax.axis_size(axis)
    forward = [(i, i + 1) for i in range(count - 1)]
    backward = [(target, source) for source, target in forward]
    return lax.ppermute(top, axis, forward), lax.ppermute(bottom, axis, backward)


def local(old_fine, coarse_fine, old_owner, new_refine, parent_map, courant):
    slabs = lax.axis_size("slab")
    tiles = lax.axis_size("tile")
    myself = lax.axis_index("tile")
    blocks, fields, cells = old_fine.shape
    per_peer = blocks // tiles
    half = E // 2

    coarse_prev = lax.ppermute(coarse_fine, "slab", [(i, (i + 1) % slabs) for i in range(slabs)])

    owner = old_owner.reshape(-1)
    slot = jnp.arange(blocks, dtype=jnp.int32)
    same = owner[:, None] == owner[None, :]
    rank = jnp.sum((same & (slot[None, :] < slot[:, None])).astype(jnp.int32), axis=1)
    position = owner * per_peer + rank
    send_idx = jnp.sum(jnp.where(position[None, :] == slot[:, None], slot[None, :], 0), axis=1)
    outgoing = old_fine[send_idx].reshape(tiles, per_peer * fields * cells // 128, 128)
    arrived = lax.all_to_all(outgoing, "tile", split_axis=0, concat_axis=0, tiled=True)
    arrived = arrived.reshape(-1, 128)
    source = (2 * myself - owner) % tiles
    inverse = source * per_peer + rank

    parents = coarse_prev[parent_map.reshape(-1)]
    parents = parents.transpose(1, 2, 0).reshape(fields, half, half, half, blocks)
    interp = refine_block_kt(parents)

    flags = new_refine.reshape(-1)
    src = jnp.where(flags == 1, blocks + slot, inverse)
    onehot = build_onehot(jnp.repeat(src, E)[None, :], 2 * blocks)
    region, ztop, zbot, ytop, ybot = assemble(arrived, interp, onehot)

    zlo, zhi = exchange(ztop, zbot, "slab")
    ylo, yhi = exchange(ytop, ybot, "tile")
    tx = xterm(courant, region)
    return advance(courant, region, zlo, zhi, ylo, yhi, tx)


def solution(mesh):
    in_specs = (
        P(("slab", "tile"), None, None),
        P(("slab", "tile"), None, None),
        P("slab", "tile", None),
        P("slab", "tile", None),
        P("slab", "tile", None),
        P(),
    )
    out_specs = P(None, "slab", "tile", None)
    return jax.shard_map(local, mesh=mesh, in_specs=in_specs, out_specs=out_specs, check_vma=False)
```

```python
import jax
import jax.numpy as jnp
from jax import lax
from jax.experimental import pallas as pl
from jax.experimental.pallas import tpu as pltpu
from jax.sharding import PartitionSpec as P

E = 8
BX = 16
BY = 4
INTERPRET = False


def slopes_kt(cells, axis):
    width = [(0, 0)] * cells.ndim
    width[axis] = (1, 1)
    padded = jnp.pad(cells, width, mode="edge")
    size = cells.shape[axis]
    below = lax.slice_in_dim(padded, 0, size, axis=axis)
    above = lax.slice_in_dim(padded, 2, size + 2, axis=axis)
    return kernel_minmod(cells - below, above - cells)


def refine_block_kt(cells):
    nd = cells.ndim
    slope_z = slopes_kt(cells, nd - 4)
    slope_y = slopes_kt(cells, nd - 3)
    slope_x = slopes_kt(cells, nd - 2)
    sigma = jnp.array([-0.25, 0.25], jnp.float32)

    def spread(value):
        return value[..., :, None, :, None, :, None, :]

    offset = (
        spread(slope_z) * sigma[:, None, None, None, None, None]
        + spread(slope_y) * sigma[:, None, None, None]
        + spread(slope_x) * sigma[:, None]
    )
    fine = spread(cells) + offset
    half = cells.shape[-2]
    return fine.reshape(cells.shape[:-4] + ((2 * half) ** 3, cells.shape[-1]))


def assemble_kernel(arr_ref, int_ref, p_ref, o_ref, zt_ref, zb_ref, yt_ref, yb_ref, at_ref):
    fields, cells, blocks = int_ref.shape
    stride = arr_ref.shape[0] // blocks
    quarters = cells // arr_ref.shape[1]
    zy = cells // E
    parts = []
    for f in range(fields):
        moved = jnp.concatenate(
            [arr_ref[pl.ds(f * quarters + q, blocks, stride=stride), :] for q in range(quarters)], axis=1)
        at_ref[f * cells:(f + 1) * cells, :blocks] = moved.T
        at_ref[f * cells:(f + 1) * cells, blocks:] = int_ref[f]
        parts.append(jnp.concatenate(
            [at_ref[pl.ds(f * cells + x, zy, stride=E), :] for x in range(E)], axis=1))
    w = jnp.concatenate(parts, axis=0)
    hi = w.astype(jnp.bfloat16)
    rest = w - hi.astype(jnp.float32)
    mid = rest.astype(jnp.bfloat16)
    lo = (rest - mid.astype(jnp.float32)).astype(jnp.bfloat16)
    res = jnp.dot(jnp.concatenate([hi, mid, lo], axis=0), p_ref[...], preferred_element_type=jnp.float32)
    n = fields * zy
    out = (res[:n] + res[n:2 * n]) + res[2 * n:]
    width = o_ref.shape[3]
    count = o_ref.shape[2] // E
    for f in range(fields):
        for by in range(count):
            piece = out[f * zy:(f + 1) * zy, by * width:(by + 1) * width].reshape(E, E, width)
            o_ref[f, :, by * E:(by + 1) * E, :] = piece
            zt_ref[f, :, by * E:(by + 1) * E, :] = piece[E - 2:]
            zb_ref[f, :, by * E:(by + 1) * E, :] = piece[:2]
            if by == 0:
                yb_ref[f] = piece[:, :2, :]
            if by == count - 1:
                yt_ref[f] = piece[:, E - 2:, :]


def onehot_kernel(src_ref, p_ref):
    rows = p_ref.shape[0] // E
    lanes = src_ref.shape[1]
    row = lax.broadcasted_iota(jnp.int32, (rows, lanes), 0)
    lane = lax.broadcasted_iota(jnp.int32, (rows, lanes), 1)
    hit = row == src_ref[...]
    for x in range(E):
        sel = hit & (lane % E == x)
        p_ref[x * rows:(x + 1) * rows, :] = jnp.where(sel, 1.0, 0.0).astype(jnp.bfloat16)


def build_onehot(srcrow, rows):
    lanes = srcrow.shape[1]
    return pl.pallas_call(
        onehot_kernel,
        out_shape=jax.ShapeDtypeStruct((E * rows, lanes), jnp.bfloat16),
        interpret=INTERPRET,
    )(srcrow)


def assemble(arrived, interp, onehot):
    fields, cells, blocks = interp.shape
    return pl.pallas_call(
        assemble_kernel,
        out_shape=[
            jax.ShapeDtypeStruct((fields, E, BY * E, BX * E), jnp.float32),
            jax.ShapeDtypeStruct((fields, 2, BY * E, BX * E), jnp.float32),
            jax.ShapeDtypeStruct((fields, 2, BY * E, BX * E), jnp.float32),
            jax.ShapeDtypeStruct((fields, E, 2, BX * E), jnp.float32),
            jax.ShapeDtypeStruct((fields, E, 2, BX * E), jnp.float32),
        ],
        scratch_shapes=[pltpu.VMEM((fields * cells, 2 * blocks), jnp.float32)],
        interpret=INTERPRET,
    )(arrived, interp, onehot)


def kernel_minmod(left, right):
    return jnp.maximum(jnp.minimum(left, right), jnp.minimum(0.0, jnp.maximum(left, right)))


def face(below, cell, above):
    return cell + 0.5 * kernel_minmod(cell - below, above - cell)


def exact_shift(v, shift):
    hi = v.astype(jnp.bfloat16)
    rest = v - hi.astype(jnp.float32)
    mid = rest.astype(jnp.bfloat16)
    lo = (rest - mid.astype(jnp.float32)).astype(jnp.bfloat16)
    n = v.shape[0]
    res = jnp.dot(jnp.concatenate([hi, mid, lo], axis=0), shift, preferred_element_type=jnp.float32)
    return (res[:n] + res[n:2 * n]) + res[2 * n:]


def xterm_kernel(c_ref, u_ref, o_ref):
    fields, zn, yn, xn = u_ref.shape
    src = lax.broadcasted_iota(jnp.int32, (xn, 2 * xn), 0)
    dst = lax.broadcasted_iota(jnp.int32, (xn, 2 * xn), 1)
    both = jnp.where(((dst < xn) & (src == dst - 1)) | ((dst >= xn) & (src == dst - xn + 1)), 1.0, 0.0)
    both = both.astype(jnp.bfloat16)
    down = both[:, :xn]
    for f in range(fields):
        cx = c_ref[2, f]
        u = u_ref[f].reshape(zn * yn, xn)
        nb = exact_shift(u, both)
        gx = face(nb[:, :xn], u, nb[:, xn:])
        gx_lo = exact_shift(gx, down)
        o_ref[f] = (cx * (gx - gx_lo)).reshape(zn, yn, xn)


def xterm(courant, region):
    vmem = pl.BlockSpec(memory_space=pltpu.VMEM)
    return pl.pallas_call(
        xterm_kernel,
        in_specs=[pl.BlockSpec(memory_space=pltpu.SMEM), vmem],
        out_specs=vmem,
        out_shape=jax.ShapeDtypeStruct(region.shape, jnp.float32),
        interpret=INTERPRET,
    )(courant, region)


def advance_kernel(c_ref, u_ref, zl_ref, zh_ref, yl_ref, yh_ref, tx_ref, o_ref):
    fields, zn, yn, xn = u_ref.shape
    lane = lax.broadcasted_iota(jnp.int32, (yn, xn), 1)
    row = lax.broadcasted_iota(jnp.int32, (yn, xn), 0)
    for f in range(fields):
        cz = c_ref[0, f]
        cy = c_ref[1, f]

        def plane(j):
            if j < 2:
                return zl_ref[f, j]
            if j < zn + 2:
                return u_ref[f, j - 2]
            return zh_ref[f, j - zn - 2]

        g_prev = face(plane(0), plane(1), plane(2))
        for z in range(zn):
            u = plane(z + 2)
            g_next = face(plane(z + 1), u, plane(z + 3))
            tz = cz * (g_next - g_prev)
            g_prev = g_next
            ylo = yl_ref[f, z]
            yhi = yh_ref[f, z]
            below = jnp.where(row == 0, ylo[1:2], pltpu.roll(u, 1, 0))
            above = jnp.where(row == yn - 1, yhi[0:1], pltpu.roll(u, yn - 1, 0))
            gy = face(below, u, above)
            gy_first = face(ylo[0:1], ylo[1:2], u[0:1])
            gy_lo = jnp.where(row == 0, gy_first, pltpu.roll(gy, 1, 0))
            ty = cy * (gy - gy_lo)
            o_ref[f, z] = u - ((tz + ty) + tx_ref[f, z])


def advance(courant, region, zlo, zhi, ylo, yhi, tx):
    vmem = pl.BlockSpec(memory_space=pltpu.VMEM)
    return pl.pallas_call(
        advance_kernel,
        in_specs=[pl.BlockSpec(memory_space=pltpu.SMEM), vmem, vmem, vmem, vmem, vmem, vmem],
        out_specs=vmem,
        out_shape=jax.ShapeDtypeStruct(region.shape, jnp.float32),
        interpret=INTERPRET,
    )(courant, region, zlo, zhi, ylo, yhi, tx)


def exchange(top, bottom, axis):
    count = lax.axis_size(axis)
    forward = [(i, i + 1) for i in range(count - 1)]
    backward = [(target, source) for source, target in forward]
    return lax.ppermute(top, axis, forward), lax.ppermute(bottom, axis, backward)


def local(old_fine, coarse_fine, old_owner, new_refine, parent_map, courant):
    slabs = lax.axis_size("slab")
    tiles = lax.axis_size("tile")
    myself = lax.axis_index("tile")
    blocks, fields, cells = old_fine.shape
    per_peer = blocks // tiles
    half = E // 2

    coarse_prev = lax.ppermute(coarse_fine, "slab", [(i, (i + 1) % slabs) for i in range(slabs)])

    owner = old_owner.reshape(-1)
    slot = jnp.arange(blocks, dtype=jnp.int32)
    same = owner[:, None] == owner[None, :]
    rank = jnp.sum((same & (slot[None, :] < slot[:, None])).astype(jnp.int32), axis=1)
    position = owner * per_peer + rank
    send_idx = jnp.sum(jnp.where(position[None, :] == slot[:, None], slot[None, :], 0), axis=1)
    outgoing = old_fine[send_idx].reshape(tiles, per_peer * fields * cells // 128, 128)
    arrived = lax.all_to_all(outgoing, "tile", split_axis=0, concat_axis=0, tiled=True)
    arrived = arrived.reshape(-1, 128)
    source = (2 * myself - owner) % tiles
    inverse = source * per_peer + rank

    parents = coarse_prev[parent_map.reshape(-1)]
    parents = parents.transpose(1, 2, 0).reshape(fields, half, half, half, blocks)
    interp = refine_block_kt(parents)

    flags = new_refine.reshape(-1)
    src = jnp.where(flags == 1, blocks + slot, inverse)
    onehot = build_onehot(jnp.repeat(src, E)[None, :], 2 * blocks)
    region, ztop, zbot, ytop, ybot = assemble(arrived, interp, onehot)

    zlo, zhi = exchange(ztop, zbot, "slab")
    ylo, yhi = exchange(ytop, ybot, "tile")
    tx = xterm(courant, region)
    return advance(courant, region, zlo, zhi, ylo, yhi, tx)


def solution(mesh):
    in_specs = (
        P(("slab", "tile"), None, None),
        P(("slab", "tile"), None, None),
        P("slab", "tile", None),
        P("slab", "tile", None),
        P("slab", "tile", None),
        P(),
    )
    out_specs = P(None, "slab", "tile", None)
    return jax.shard_map(local, mesh=mesh, in_specs=in_specs, out_specs=out_specs, check_vma=False)
```

```python
import jax
import jax.numpy as jnp
from jax import lax
from jax.experimental import pallas as pl
from jax.experimental.pallas import tpu as pltpu
from jax.sharding import PartitionSpec as P

E = 8
BX = 16
BY = 4
INTERPRET = False


def slopes_kt(cells, axis):
    width = [(0, 0)] * cells.ndim
    width[axis] = (1, 1)
    padded = jnp.pad(cells, width, mode="edge")
    size = cells.shape[axis]
    below = lax.slice_in_dim(padded, 0, size, axis=axis)
    above = lax.slice_in_dim(padded, 2, size + 2, axis=axis)
    return kernel_minmod(cells - below, above - cells)


def refine_block_kt(cells):
    nd = cells.ndim
    slope_z = slopes_kt(cells, nd - 4)
    slope_y = slopes_kt(cells, nd - 3)
    slope_x = slopes_kt(cells, nd - 2)
    sigma = jnp.array([-0.25, 0.25], jnp.float32)

    def spread(value):
        return value[..., :, None, :, None, :, None, :]

    offset = (
        spread(slope_z) * sigma[:, None, None, None, None, None]
        + spread(slope_y) * sigma[:, None, None, None]
        + spread(slope_x) * sigma[:, None]
    )
    fine = spread(cells) + offset
    half = cells.shape[-2]
    return fine.reshape(cells.shape[:-4] + ((2 * half) ** 3, cells.shape[-1]))


def assemble_kernel(arr_ref, int_ref, p_ref, o_ref, zt_ref, zb_ref, yt_ref, yb_ref, at_ref):
    fields, cells, blocks = int_ref.shape
    stride = arr_ref.shape[0] // blocks
    quarters = cells // arr_ref.shape[1]
    zy = cells // E
    parts = []
    for f in range(fields):
        moved = jnp.concatenate(
            [arr_ref[pl.ds(f * quarters + q, blocks, stride=stride), :] for q in range(quarters)], axis=1)
        at_ref[f * cells:(f + 1) * cells, :blocks] = moved.T
        at_ref[f * cells:(f + 1) * cells, blocks:] = int_ref[f]
        parts.append(jnp.concatenate(
            [at_ref[pl.ds(f * cells + x, zy, stride=E), :] for x in range(E)], axis=1))
    w = jnp.concatenate(parts, axis=0)
    hi = w.astype(jnp.bfloat16)
    mid = (w - hi.astype(jnp.float32)).astype(jnp.bfloat16)
    res = jnp.dot(jnp.concatenate([hi, mid], axis=0), p_ref[...], preferred_element_type=jnp.float32)
    n = fields * zy
    out = res[:n] + res[n:]
    width = o_ref.shape[3]
    count = o_ref.shape[2] // E
    for f in range(fields):
        for by in range(count):
            piece = out[f * zy:(f + 1) * zy, by * width:(by + 1) * width].reshape(E, E, width)
            o_ref[f, :, by * E:(by + 1) * E, :] = piece
            zt_ref[f, :, by * E:(by + 1) * E, :] = piece[E - 2:]
            zb_ref[f, :, by * E:(by + 1) * E, :] = piece[:2]
            if by == 0:
                yb_ref[f] = piece[:, :2, :]
            if by == count - 1:
                yt_ref[f] = piece[:, E - 2:, :]


def onehot_kernel(src_ref, p_ref):
    rows = p_ref.shape[0] // E
    lanes = src_ref.shape[1]
    row = lax.broadcasted_iota(jnp.int32, (rows, lanes), 0)
    lane = lax.broadcasted_iota(jnp.int32, (rows, lanes), 1)
    hit = row == src_ref[...]
    for x in range(E):
        sel = hit & (lane % E == x)
        p_ref[x * rows:(x + 1) * rows, :] = jnp.where(sel, 1.0, 0.0).astype(jnp.bfloat16)


def build_onehot(srcrow, rows):
    lanes = srcrow.shape[1]
    return pl.pallas_call(
        onehot_kernel,
        out_shape=jax.ShapeDtypeStruct((E * rows, lanes), jnp.bfloat16),
        interpret=INTERPRET,
    )(srcrow)


def assemble(arrived, interp, onehot):
    fields, cells, blocks = interp.shape
    return pl.pallas_call(
        assemble_kernel,
        out_shape=[
            jax.ShapeDtypeStruct((fields, E, BY * E, BX * E), jnp.float32),
            jax.ShapeDtypeStruct((fields, 2, BY * E, BX * E), jnp.float32),
            jax.ShapeDtypeStruct((fields, 2, BY * E, BX * E), jnp.float32),
            jax.ShapeDtypeStruct((fields, E, 2, BX * E), jnp.float32),
            jax.ShapeDtypeStruct((fields, E, 2, BX * E), jnp.float32),
        ],
        scratch_shapes=[pltpu.VMEM((fields * cells, 2 * blocks), jnp.float32)],
        interpret=INTERPRET,
    )(arrived, interp, onehot)


def kernel_minmod(left, right):
    return jnp.maximum(jnp.minimum(left, right), jnp.minimum(0.0, jnp.maximum(left, right)))


def face(below, cell, above):
    return cell + 0.5 * kernel_minmod(cell - below, above - cell)


def exact_shift(v, shift):
    hi = v.astype(jnp.bfloat16)
    rest = v - hi.astype(jnp.float32)
    mid = rest.astype(jnp.bfloat16)
    lo = (rest - mid.astype(jnp.float32)).astype(jnp.bfloat16)
    n = v.shape[0]
    res = jnp.dot(jnp.concatenate([hi, mid, lo], axis=0), shift, preferred_element_type=jnp.float32)
    return (res[:n] + res[n:2 * n]) + res[2 * n:]


def xterm_kernel(c_ref, u_ref, o_ref):
    fields, zn, yn, xn = u_ref.shape
    src = lax.broadcasted_iota(jnp.int32, (xn, 2 * xn), 0)
    dst = lax.broadcasted_iota(jnp.int32, (xn, 2 * xn), 1)
    both = jnp.where(((dst < xn) & (src == dst - 1)) | ((dst >= xn) & (src == dst - xn + 1)), 1.0, 0.0)
    both = both.astype(jnp.bfloat16)
    down = both[:, :xn]
    for f in range(fields):
        cx = c_ref[2, f]
        u = u_ref[f].reshape(zn * yn, xn)
        nb = exact_shift(u, both)
        gx = face(nb[:, :xn], u, nb[:, xn:])
        gx_lo = exact_shift(gx, down)
        o_ref[f] = (cx * (gx - gx_lo)).reshape(zn, yn, xn)


def xterm(courant, region):
    vmem = pl.BlockSpec(memory_space=pltpu.VMEM)
    return pl.pallas_call(
        xterm_kernel,
        in_specs=[pl.BlockSpec(memory_space=pltpu.SMEM), vmem],
        out_specs=vmem,
        out_shape=jax.ShapeDtypeStruct(region.shape, jnp.float32),
        interpret=INTERPRET,
    )(courant, region)


def advance_kernel(c_ref, u_ref, zl_ref, zh_ref, yl_ref, yh_ref, tx_ref, o_ref):
    fields, zn, yn, xn = u_ref.shape
    lane = lax.broadcasted_iota(jnp.int32, (yn, xn), 1)
    row = lax.broadcasted_iota(jnp.int32, (yn, xn), 0)
    for f in range(fields):
        cz = c_ref[0, f]
        cy = c_ref[1, f]

        def plane(j):
            if j < 2:
                return zl_ref[f, j]
            if j < zn + 2:
                return u_ref[f, j - 2]
            return zh_ref[f, j - zn - 2]

        g_prev = face(plane(0), plane(1), plane(2))
        for z in range(zn):
            u = plane(z + 2)
            g_next = face(plane(z + 1), u, plane(z + 3))
            tz = cz * (g_next - g_prev)
            g_prev = g_next
            ylo = yl_ref[f, z]
            yhi = yh_ref[f, z]
            below = jnp.where(row == 0, ylo[1:2], pltpu.roll(u, 1, 0))
            above = jnp.where(row == yn - 1, yhi[0:1], pltpu.roll(u, yn - 1, 0))
            gy = face(below, u, above)
            gy_first = face(ylo[0:1], ylo[1:2], u[0:1])
            gy_lo = jnp.where(row == 0, gy_first, pltpu.roll(gy, 1, 0))
            ty = cy * (gy - gy_lo)
            o_ref[f, z] = u - ((tz + ty) + tx_ref[f, z])


def advance(courant, region, zlo, zhi, ylo, yhi, tx):
    vmem = pl.BlockSpec(memory_space=pltpu.VMEM)
    return pl.pallas_call(
        advance_kernel,
        in_specs=[pl.BlockSpec(memory_space=pltpu.SMEM), vmem, vmem, vmem, vmem, vmem, vmem],
        out_specs=vmem,
        out_shape=jax.ShapeDtypeStruct(region.shape, jnp.float32),
        interpret=INTERPRET,
    )(courant, region, zlo, zhi, ylo, yhi, tx)


def exchange(top, bottom, axis):
    count = lax.axis_size(axis)
    forward = [(i, i + 1) for i in range(count - 1)]
    backward = [(target, source) for source, target in forward]
    return lax.ppermute(top, axis, forward), lax.ppermute(bottom, axis, backward)


def local(old_fine, coarse_fine, old_owner, new_refine, parent_map, courant):
    slabs = lax.axis_size("slab")
    tiles = lax.axis_size("tile")
    myself = lax.axis_index("tile")
    blocks, fields, cells = old_fine.shape
    per_peer = blocks // tiles
    half = E // 2

    coarse_prev = lax.ppermute(coarse_fine, "slab", [(i, (i + 1) % slabs) for i in range(slabs)])

    owner = old_owner.reshape(-1)
    slot = jnp.arange(blocks, dtype=jnp.int32)
    same = owner[:, None] == owner[None, :]
    rank = jnp.sum((same & (slot[None, :] < slot[:, None])).astype(jnp.int32), axis=1)
    position = owner * per_peer + rank
    send_idx = jnp.sum(jnp.where(position[None, :] == slot[:, None], slot[None, :], 0), axis=1)
    outgoing = old_fine[send_idx].reshape(tiles, per_peer * fields * cells // 128, 128)
    arrived = lax.all_to_all(outgoing, "tile", split_axis=0, concat_axis=0, tiled=True)
    arrived = arrived.reshape(-1, 128)
    source = (2 * myself - owner) % tiles
    inverse = source * per_peer + rank

    parents = coarse_prev[parent_map.reshape(-1)]
    parents = parents.transpose(1, 2, 0).reshape(fields, half, half, half, blocks)
    interp = refine_block_kt(parents)

    flags = new_refine.reshape(-1)
    src = jnp.where(flags == 1, blocks + slot, inverse)
    onehot = build_onehot(jnp.repeat(src, E)[None, :], 2 * blocks)
    region, ztop, zbot, ytop, ybot = assemble(arrived, interp, onehot)

    zlo, zhi = exchange(ztop, zbot, "slab")
    ylo, yhi = exchange(ytop, ybot, "tile")
    tx = xterm(courant, region)
    return advance(courant, region, zlo, zhi, ylo, yhi, tx)


def solution(mesh):
    in_specs = (
        P(("slab", "tile"), None, None),
        P(("slab", "tile"), None, None),
        P("slab", "tile", None),
        P("slab", "tile", None),
        P("slab", "tile", None),
        P(),
    )
    out_specs = P(None, "slab", "tile", None)
    return jax.shard_map(local, mesh=mesh, in_specs=in_specs, out_specs=out_specs, check_vma=False)
```

```python
import jax
import jax.numpy as jnp
from jax import lax
from jax.experimental import pallas as pl
from jax.experimental.pallas import tpu as pltpu
from jax.sharding import PartitionSpec as P

E = 8
BX = 16
BY = 4
INTERPRET = False


def slopes_kt(cells, axis):
    width = [(0, 0)] * cells.ndim
    width[axis] = (1, 1)
    padded = jnp.pad(cells, width, mode="edge")
    size = cells.shape[axis]
    below = lax.slice_in_dim(padded, 0, size, axis=axis)
    above = lax.slice_in_dim(padded, 2, size + 2, axis=axis)
    return kernel_minmod(cells - below, above - cells)


def refine_block_kt(cells):
    nd = cells.ndim
    slope_z = slopes_kt(cells, nd - 4)
    slope_y = slopes_kt(cells, nd - 3)
    slope_x = slopes_kt(cells, nd - 2)
    sigma = jnp.array([-0.25, 0.25], jnp.float32)

    def spread(value):
        return value[..., :, None, :, None, :, None, :]

    offset = (
        spread(slope_z) * sigma[:, None, None, None, None, None]
        + spread(slope_y) * sigma[:, None, None, None]
        + spread(slope_x) * sigma[:, None]
    )
    fine = spread(cells) + offset
    half = cells.shape[-2]
    return fine.reshape(cells.shape[:-4] + ((2 * half) ** 3, cells.shape[-1]))


def assemble_kernel(arr_ref, int_ref, p_ref, o_ref, zt_ref, zb_ref, yt_ref, yb_ref, at_ref):
    fields, cells, blocks = int_ref.shape
    stride = arr_ref.shape[0] // blocks
    quarters = cells // arr_ref.shape[1]
    zy = cells // E
    parts = []
    for f in range(fields):
        moved = jnp.concatenate(
            [arr_ref[pl.ds(f * quarters + q, blocks, stride=stride), :] for q in range(quarters)], axis=1)
        at_ref[f * cells:(f + 1) * cells, :blocks] = moved.T
        at_ref[f * cells:(f + 1) * cells, blocks:] = int_ref[f]
        parts.append(jnp.concatenate(
            [at_ref[pl.ds(f * cells + x, zy, stride=E), :] for x in range(E)], axis=1))
    w = jnp.concatenate(parts, axis=0)
    hi = w.astype(jnp.bfloat16)
    mid = (w - hi.astype(jnp.float32)).astype(jnp.bfloat16)
    res = jnp.dot(jnp.concatenate([hi, mid], axis=0), p_ref[...], preferred_element_type=jnp.float32)
    n = fields * zy
    out = res[:n] + res[n:]
    width = o_ref.shape[3]
    count = o_ref.shape[2] // E
    for f in range(fields):
        for by in range(count):
            piece = out[f * zy:(f + 1) * zy, by * width:(by + 1) * width].reshape(E, E, width)
            o_ref[f, :, by * E:(by + 1) * E, :] = piece
            zt_ref[f, :, by * E:(by + 1) * E, :] = piece[E - 2:]
            zb_ref[f, :, by * E:(by + 1) * E, :] = piece[:2]
            if by == 0:
                yb_ref[f] = piece[:, :2, :]
            if by == count - 1:
                yt_ref[f] = piece[:, E - 2:, :]


def onehot_kernel(src_ref, p_ref):
    rows = p_ref.shape[0] // E
    lanes = src_ref.shape[1]
    row = lax.broadcasted_iota(jnp.int32, (rows, lanes), 0)
    lane = lax.broadcasted_iota(jnp.int32, (rows, lanes), 1)
    hit = row == src_ref[...]
    for x in range(E):
        sel = hit & (lane % E == x)
        p_ref[x * rows:(x + 1) * rows, :] = jnp.where(sel, 1.0, 0.0).astype(jnp.bfloat16)


def build_onehot(srcrow, rows):
    lanes = srcrow.shape[1]
    return pl.pallas_call(
        onehot_kernel,
        out_shape=jax.ShapeDtypeStruct((E * rows, lanes), jnp.bfloat16),
        interpret=INTERPRET,
    )(srcrow)


def assemble(arrived, interp, onehot):
    fields, cells, blocks = interp.shape
    return pl.pallas_call(
        assemble_kernel,
        out_shape=[
            jax.ShapeDtypeStruct((fields, E, BY * E, BX * E), jnp.float32),
            jax.ShapeDtypeStruct((fields, 2, BY * E, BX * E), jnp.float32),
            jax.ShapeDtypeStruct((fields, 2, BY * E, BX * E), jnp.float32),
            jax.ShapeDtypeStruct((fields, E, 2, BX * E), jnp.float32),
            jax.ShapeDtypeStruct((fields, E, 2, BX * E), jnp.float32),
        ],
        scratch_shapes=[pltpu.VMEM((fields * cells, 2 * blocks), jnp.float32)],
        interpret=INTERPRET,
    )(arrived, interp, onehot)


def kernel_minmod(left, right):
    return jnp.maximum(jnp.minimum(left, right), jnp.minimum(0.0, jnp.maximum(left, right)))


def face(below, cell, above):
    return cell + 0.5 * kernel_minmod(cell - below, above - cell)


def exact_shift(v, shift):
    hi = v.astype(jnp.bfloat16)
    mid = (v - hi.astype(jnp.float32)).astype(jnp.bfloat16)
    n = v.shape[0]
    res = jnp.dot(jnp.concatenate([hi, mid], axis=0), shift, preferred_element_type=jnp.float32)
    return res[:n] + res[n:]


def xterm_kernel(c_ref, u_ref, o_ref):
    fields, zn, yn, xn = u_ref.shape
    src = lax.broadcasted_iota(jnp.int32, (xn, 2 * xn), 0)
    dst = lax.broadcasted_iota(jnp.int32, (xn, 2 * xn), 1)
    both = jnp.where(((dst < xn) & (src == dst - 1)) | ((dst >= xn) & (src == dst - xn + 1)), 1.0, 0.0)
    both = both.astype(jnp.bfloat16)
    down = both[:, :xn]
    for f in range(fields):
        cx = c_ref[2, f]
        u = u_ref[f].reshape(zn * yn, xn)
        nb = exact_shift(u, both)
        gx = face(nb[:, :xn], u, nb[:, xn:])
        gx_lo = exact_shift(gx, down)
        o_ref[f] = (cx * (gx - gx_lo)).reshape(zn, yn, xn)


def xterm(courant, region):
    vmem = pl.BlockSpec(memory_space=pltpu.VMEM)
    return pl.pallas_call(
        xterm_kernel,
        in_specs=[pl.BlockSpec(memory_space=pltpu.SMEM), vmem],
        out_specs=vmem,
        out_shape=jax.ShapeDtypeStruct(region.shape, jnp.float32),
        interpret=INTERPRET,
    )(courant, region)


def advance_kernel(c_ref, u_ref, zl_ref, zh_ref, yl_ref, yh_ref, tx_ref, o_ref):
    fields, zn, yn, xn = u_ref.shape
    lane = lax.broadcasted_iota(jnp.int32, (yn, xn), 1)
    row = lax.broadcasted_iota(jnp.int32, (yn, xn), 0)
    for f in range(fields):
        cz = c_ref[0, f]
        cy = c_ref[1, f]

        def plane(j):
            if j < 2:
                return zl_ref[f, j]
            if j < zn + 2:
                return u_ref[f, j - 2]
            return zh_ref[f, j - zn - 2]

        g_prev = face(plane(0), plane(1), plane(2))
        for z in range(zn):
            u = plane(z + 2)
            g_next = face(plane(z + 1), u, plane(z + 3))
            tz = cz * (g_next - g_prev)
            g_prev = g_next
            ylo = yl_ref[f, z]
            yhi = yh_ref[f, z]
            below = jnp.where(row == 0, ylo[1:2], pltpu.roll(u, 1, 0))
            above = jnp.where(row == yn - 1, yhi[0:1], pltpu.roll(u, yn - 1, 0))
            gy = face(below, u, above)
            gy_first = face(ylo[0:1], ylo[1:2], u[0:1])
            gy_lo = jnp.where(row == 0, gy_first, pltpu.roll(gy, 1, 0))
            ty = cy * (gy - gy_lo)
            o_ref[f, z] = u - ((tz + ty) + tx_ref[f, z])


def advance(courant, region, zlo, zhi, ylo, yhi, tx):
    vmem = pl.BlockSpec(memory_space=pltpu.VMEM)
    return pl.pallas_call(
        advance_kernel,
        in_specs=[pl.BlockSpec(memory_space=pltpu.SMEM), vmem, vmem, vmem, vmem, vmem, vmem],
        out_specs=vmem,
        out_shape=jax.ShapeDtypeStruct(region.shape, jnp.float32),
        interpret=INTERPRET,
    )(courant, region, zlo, zhi, ylo, yhi, tx)


def exchange(top, bottom, axis):
    count = lax.axis_size(axis)
    forward = [(i, i + 1) for i in range(count - 1)]
    backward = [(target, source) for source, target in forward]
    return lax.ppermute(top, axis, forward), lax.ppermute(bottom, axis, backward)


def local(old_fine, coarse_fine, old_owner, new_refine, parent_map, courant):
    slabs = lax.axis_size("slab")
    tiles = lax.axis_size("tile")
    myself = lax.axis_index("tile")
    blocks, fields, cells = old_fine.shape
    per_peer = blocks // tiles
    half = E // 2

    coarse_prev = lax.ppermute(coarse_fine, "slab", [(i, (i + 1) % slabs) for i in range(slabs)])

    owner = old_owner.reshape(-1)
    slot = jnp.arange(blocks, dtype=jnp.int32)
    same = owner[:, None] == owner[None, :]
    rank = jnp.sum((same & (slot[None, :] < slot[:, None])).astype(jnp.int32), axis=1)
    position = owner * per_peer + rank
    send_idx = jnp.sum(jnp.where(position[None, :] == slot[:, None], slot[None, :], 0), axis=1)
    outgoing = old_fine[send_idx].reshape(tiles, per_peer * fields * cells // 128, 128)
    arrived = lax.all_to_all(outgoing, "tile", split_axis=0, concat_axis=0, tiled=True)
    arrived = arrived.reshape(-1, 128)
    source = (2 * myself - owner) % tiles
    inverse = source * per_peer + rank

    parents = coarse_prev[parent_map.reshape(-1)]
    parents = parents.transpose(1, 2, 0).reshape(fields, half, half, half, blocks)
    interp = refine_block_kt(parents)

    flags = new_refine.reshape(-1)
    src = jnp.where(flags == 1, blocks + slot, inverse)
    onehot = build_onehot(jnp.repeat(src, E)[None, :], 2 * blocks)
    region, ztop, zbot, ytop, ybot = assemble(arrived, interp, onehot)

    zlo, zhi = exchange(ztop, zbot, "slab")
    ylo, yhi = exchange(ytop, ybot, "tile")
    tx = xterm(courant, region)
    return advance(courant, region, zlo, zhi, ylo, yhi, tx)


def solution(mesh):
    in_specs = (
        P(("slab", "tile"), None, None),
        P(("slab", "tile"), None, None),
        P("slab", "tile", None),
        P("slab", "tile", None),
        P("slab", "tile", None),
        P(),
    )
    out_specs = P(None, "slab", "tile", None)
    return jax.shard_map(local, mesh=mesh, in_specs=in_specs, out_specs=out_specs, check_vma=False)
```
